256 devices in a mesh: row: 16 (over y_hi, x, core), col: 16 (over z, y_lo).
Axes of the slice: x: 4, y: 4 (y_hi: 2, y_lo: 2; y = y_hi * 2 + y_lo), z: 8, core: 2. Of those that a mesh axis runs over, the one named last changes fastest.
Arguments:
- data_rows: bfloat16 [393216, 256], P(('row', 'col')), may hold values from -7 to 7
- data_mass: float32 [393216], P(('row', 'col')), may hold values from 0.3 to 3
- block_links: int32 [3072, 16], P(('row', 'col')), may hold values from 0 to 31, all different within a row
- cand_rows: bfloat16 [4096, 256], P('col'), may hold values from -7 to 7
- cand_mass: float32 [4096], replicated, may hold values from 0.3 to 3
Outputs:
- data_scale: float32 [393216], P(('row', 'col'))
- cand_scale: float32 [4096], P('col')
- new_support: float32 [4096, 256], P('col')
The draws below stay inside these ranges and needn't reach their ends.
Inputs may be any that keep to these rules, and one draw needn't show every extreme that they name: `block_links`: each row names 16 different candidate blocks; every candidate block is named by some row.
All inputs are finite; a program needn't handle non-finite values.
Results may differ from the reference program's by a relative error of at most 0.0014.
Values may be sent and summed in bfloat16 or wider, within the bound.
No kernel may reach another device: no remote copies, remote signals or barrier semaphores. Data moves between devices by JAX's collectives and lax.ppermute only.
A program may use at most 64 MiB of HBM per device.

```python
import math
import jax
import jax.numpy as jnp
from jax import lax

D = 256
BLOCK = 128
NBR = 16
ITERS = 3
R_DEV = 1536
NDATA = 393216
NCAND = 4096
NDB = 3072


SHIFT = 0.26


LEVEL = 1.6


def shared_direction(key):
    return jax.random.rademacher(jax.random.fold_in(key, 7001), (D,)).astype(jnp.float32)


def span_signs(key):
    signs = jax.random.rademacher(jax.random.fold_in(key, 7002), (NDATA // R_DEV,)).astype(jnp.float32)
    return jnp.repeat(signs, R_DEV, total_repeat_length=NDATA)


def candidate_signs(key):
    return jax.random.rademacher(jax.random.fold_in(key, 7003), (NCAND,)).astype(jnp.float32)


def log_between(key, count, lower, upper):
    spread = jax.random.uniform(key, (count,), jnp.float32)
    return jnp.exp(math.log(lower) + spread * (math.log(upper) - math.log(lower)))


def draw_data_rows(key, part):
    direction = shared_direction(key)
    signs = span_signs(key)
    noise = jax.random.normal(jax.random.fold_in(key, 7011), (NDATA, D), jnp.float32)
    shift = SHIFT
    rows = jnp.clip(noise + shift * signs[:, None] * direction[None, :], -7.0, 7.0)
    return rows.astype(jnp.bfloat16)


def draw_cand_rows(key, part):
    direction = shared_direction(key)
    signs = candidate_signs(key)
    noise = jax.random.normal(jax.random.fold_in(key, 7012), (NCAND, D), jnp.float32)
    shift = SHIFT
    rows = jnp.clip(noise + shift * signs[:, None] * direction[None, :], -7.0, 7.0)
    return rows.astype(jnp.bfloat16)


def draw_data_mass(key, part):
    base = log_between(jax.random.fold_in(key, 7021), NDATA, 0.5, 1.85)
    return (base * jnp.exp(span_signs(key) * math.log(LEVEL))).astype(jnp.float32)


def draw_cand_mass(key, part):
    base = log_between(jax.random.fold_in(key, 7022), NCAND, 0.5, 1.85)
    return (base * jnp.exp(-candidate_signs(key) * math.log(LEVEL))).astype(jnp.float32)


def picks_of(rng, rows, amount, top, lift):
    sequence = jax.random.permutation(jax.random.fold_in(rng, 1), amount)
    favour = sequence
    for power in range(3):
        favour = favour * favour // amount
    favour = favour * lift // amount
    lots = jax.random.randint(jax.random.fold_in(rng, 2), (rows, amount), 0, 4096) + favour
    holders = jax.random.permutation(jax.random.fold_in(rng, 3), rows)[jnp.arange(amount) % rows]
    lots = jnp.where(jnp.arange(rows)[:, None] == holders[None, :], 1 << 14, lots)
    priority = lots * amount + jnp.arange(amount)
    return lax.top_k(priority.astype(jnp.int32), top)[1].astype(jnp.int32)


def setup_inputs(seed: int = 0) -> dict:
    splits = jax.random.split(jax.random.key(seed), 6)
    data_rows = draw_data_rows(jax.random.fold_in(splits[5], 71), 0)
    data_mass = draw_data_mass(jax.random.fold_in(splits[5], 71), 0)
    block_links = picks_of(splits[2], NDB, NCAND // BLOCK, NBR, 8192)
    cand_rows = draw_cand_rows(jax.random.fold_in(splits[5], 71), 0)
    cand_mass = draw_cand_mass(jax.random.fold_in(splits[5], 71), 0)
    return dict(data_rows=data_rows, data_mass=data_mass, block_links=block_links, cand_rows=cand_rows, cand_mass=cand_mass)


EPS = 0.05
OFFSET = 1.0

def normalize(matrix):
    values = matrix.astype(jnp.float32)
    return (values * lax.rsqrt(lax.optimization_barrier(jnp.mean(values * values, axis=1, keepdims=True)) + 1e-06)).astype(jnp.bfloat16)

def kernel_tiles(data_group, cand_blocks, link_group):
    feature_count = data_group.shape[-1]
    chosen = cand_blocks[link_group].reshape(link_group.shape[0], -1, feature_count)
    scores = jnp.einsum('gid,gjd->gij', data_group.astype(jnp.float32), chosen.astype(jnp.float32))
    return jnp.exp(scores * (1.0 / (feature_count * EPS)) - OFFSET) * (1.0 / chosen.shape[1])

def row_update(kernel_tile, link_group, scale_blocks, mass_group):
    linked_scale = scale_blocks[link_group].reshape(link_group.shape[0], -1)
    row_total = lax.optimization_barrier(jnp.sum(kernel_tile * linked_scale[:, None, :], axis=2))
    return mass_group / row_total

def column_part(kernel_tile, link_group, scale_rows, block_count):
    slot_mass = lax.optimization_barrier(jnp.sum(kernel_tile * scale_rows[:, :, None], axis=1)).reshape(-1, BLOCK)
    return jax.ops.segment_sum(slot_mass, link_group.reshape(-1), num_segments=block_count)

def weighted_part(kernel_tile, link_group, scale_rows, rows_group, block_count):
    plan_weights = (kernel_tile * scale_rows[:, :, None]).astype(jnp.bfloat16)
    slot_sums = jnp.einsum('gij,gid->gjd', plan_weights.astype(jnp.float32), rows_group.astype(jnp.float32))
    slot_sums = slot_sums.reshape(-1, BLOCK, rows_group.shape[-1])
    return jax.ops.segment_sum(slot_sums, link_group.reshape(-1), num_segments=block_count)

def reference(data_rows, data_mass, block_links, cand_rows, cand_mass):
    block_count = NCAND // BLOCK
    group_size = min(4, R_DEV // BLOCK)
    group_count = NDATA // (BLOCK * group_size)
    cand_blocks = normalize(cand_rows).reshape(block_count, BLOCK, D)
    data_groups = normalize(data_rows).reshape(group_count, group_size, BLOCK, D)
    rows_groups = data_rows.reshape(group_count, group_size, BLOCK, D)
    mass_groups = data_mass.reshape(group_count, group_size, BLOCK)
    link_groups = block_links.reshape(group_count, group_size, NBR)
    mass_ratio = NDATA / NCAND
    scale_blocks = jnp.ones((block_count, BLOCK), jnp.float32)
    column_total = jnp.zeros((block_count, BLOCK), jnp.float32)
    scale_rows = jnp.zeros((group_count, group_size, BLOCK), jnp.float32)
    for sweep_index in range(ITERS):

        def sweep_step(running, inputs):
            data_group, mass_group, link_group = inputs
            kernel_tile = kernel_tiles(data_group, cand_blocks, link_group)
            new_scale = row_update(kernel_tile, link_group, scale_blocks, mass_group)
            return (running + column_part(kernel_tile, link_group, new_scale, block_count), new_scale)
        column_total, scale_rows = lax.scan(sweep_step, jnp.zeros((block_count, BLOCK), jnp.float32), (data_groups, mass_groups, link_groups))
        scale_blocks = mass_ratio * cand_mass.reshape(block_count, BLOCK) / column_total

    def bary_step(running, inputs):
        data_group, rows_group, link_group, scale_group = inputs
        kernel_tile = kernel_tiles(data_group, cand_blocks, link_group)
        return (running + weighted_part(kernel_tile, link_group, scale_group, rows_group, block_count), None)
    weighted_sums, unused = lax.scan(bary_step, jnp.zeros((block_count, BLOCK, D), jnp.float32), (data_groups, rows_groups, link_groups, scale_rows))
    new_support = weighted_sums.reshape(NCAND, D) / column_total.reshape(NCAND, 1)
    return (scale_rows.reshape(NDATA), scale_blocks.reshape(NCAND), new_support)
```

```python
import functools

import jax
import jax.numpy as jnp
from jax import lax
from jax.experimental import pallas as pl
from jax.experimental.pallas import tpu as pltpu
from jax.sharding import Mesh
from jax.sharding import PartitionSpec as P

BLOCK = 128
ITERS = 3


EPS = 0.05
OFFSET = 1.0

ROW_AXES = ("yh", "x", "c")
COL_AXES = ("z", "yl")
ALL_AXES = ROW_AXES + COL_AXES


def normalize(matrix):
    values = matrix.astype(jnp.float32)
    return (values * lax.rsqrt(jnp.mean(values * values, axis=1, keepdims=True) + 1e-06)).astype(
        jnp.bfloat16
    )


def butterfly_sum(x, sizes):
    for axis in ALL_AXES:
        n = sizes[axis]
        k = 1
        while k < n:
            x = x + lax.ppermute(x, axis, [(j, j ^ k) for j in range(n)])
            k *= 2
    return x


def _kernel_slot(xn, cn_ref, blk, inv_width, inv_count):
    cand = cn_ref[blk]
    scores = lax.dot_general(
        xn, cand, (((1,), (1,)), ((), ())), preferred_element_type=jnp.float32
    )
    return jnp.exp(scores * inv_width - OFFSET) * inv_count


def sweep_body(nbr, inv_width, inv_count, bary, links_ref, xn_ref, cn_ref, scale_ref, mass_ref,
               *rest):
    if bary:
        rows_ref, ds_ref, ct_ref, ws_ref, kbuf = rest
    else:
        ds_ref, ct_ref, kbuf = rest
    b = pl.program_id(0)

    @pl.when(b == 0)
    def _():
        ct_ref[...] = jnp.zeros_like(ct_ref)
        if bary:
            ws_ref[...] = jnp.zeros_like(ws_ref)

    xn = xn_ref[...]
    acc = jnp.zeros((BLOCK, BLOCK), jnp.float32)
    for s in range(nbr):
        blk = links_ref[b, s]
        k = _kernel_slot(xn, cn_ref, blk, inv_width, inv_count)
        kbuf[s] = k
        acc = acc + k * scale_ref[pl.ds(blk, 1), :]
    row_total = jnp.sum(acc, axis=1, keepdims=True)
    ds = mass_ref[...] / row_total
    ds_ref[...] = ds
    if bary:
        rows = rows_ref[...]
    for s in range(nbr):
        blk = links_ref[b, s]
        k = kbuf[s]
        part = jnp.sum(k * ds, axis=0, keepdims=True)
        ct_ref[pl.ds(blk, 1), :] += part
        if bary:
            w = (k * ds).astype(jnp.bfloat16)
            ws_ref[blk] += lax.dot_general(
                w, rows, (((0,), (0,)), ((), ())), preferred_element_type=jnp.float32
            )


def sweep(xn, cn_blocks, scale_blocks, mass_col, links, rows=None):
    local_rows, feature_count = xn.shape
    block_count = cn_blocks.shape[0]
    local_blocks, nbr = links.shape
    bary = rows is not None
    inv_width = 1.0 / (feature_count * EPS)
    inv_count = 1.0 / (nbr * BLOCK)
    in_specs = [
        pl.BlockSpec((BLOCK, feature_count), lambda b, L: (b, 0)),
        pl.BlockSpec((block_count, BLOCK, feature_count), lambda b, L: (0, 0, 0)),
        pl.BlockSpec((block_count, BLOCK), lambda b, L: (0, 0)),
        pl.BlockSpec((BLOCK, 1), lambda b, L: (b, 0)),
    ]
    out_specs = [
        pl.BlockSpec((BLOCK, 1), lambda b, L: (b, 0)),
        pl.BlockSpec((block_count, BLOCK), lambda b, L: (0, 0)),
    ]
    out_shape = [
        jax.ShapeDtypeStruct((local_rows, 1), jnp.float32),
        jax.ShapeDtypeStruct((block_count, BLOCK), jnp.float32),
    ]
    args = [links, xn, cn_blocks, scale_blocks, mass_col]
    if bary:
        in_specs.append(pl.BlockSpec((BLOCK, feature_count), lambda b, L: (b, 0)))
        out_specs.append(
            pl.BlockSpec((block_count, BLOCK, feature_count), lambda b, L: (0, 0, 0))
        )
        out_shape.append(jax.ShapeDtypeStruct((block_count, BLOCK, feature_count), jnp.float32))
        args.append(rows)
    flops = 2 * local_rows * nbr * BLOCK * feature_count * (2 if bary else 1)
    return pl.pallas_call(
        functools.partial(sweep_body, nbr, inv_width, inv_count, bary),
        grid_spec=pltpu.PrefetchScalarGridSpec(
            num_scalar_prefetch=1,
            grid=(local_blocks,),
            in_specs=in_specs,
            out_specs=out_specs,
            scratch_shapes=[pltpu.VMEM((nbr, BLOCK, BLOCK), jnp.float32)],
        ),
        out_shape=out_shape,
        compiler_params=pltpu.CompilerParams(
            dimension_semantics=("arbitrary",), vmem_limit_bytes=48 * 1024 * 1024
        ),
        cost_estimate=pl.CostEstimate(
            flops=flops,
            transcendentals=local_rows * nbr * BLOCK,
            bytes_accessed=block_count * BLOCK * feature_count * (2 + (4 if bary else 0))
            + local_rows * feature_count * (4 if bary else 2),
        ),
    )(*args)


def on_device(sizes, data_rows, data_mass, block_links, cand_rows, cand_mass):
    local_rows, feature_count = data_rows.shape
    local_cands = cand_rows.shape[0]
    row_devices = sizes["yh"] * sizes["x"] * sizes["c"]
    col_devices = sizes["z"] * sizes["yl"]
    cand_total = local_cands * col_devices
    block_count = cand_total // BLOCK
    mass_ratio = local_rows * row_devices / local_cands
    col_index = lax.axis_index("z") * sizes["yl"] + lax.axis_index("yl")
    own_start = col_index * local_cands
    gathered = lax.all_gather(normalize(cand_rows), COL_AXES, axis=0, tiled=True)
    cn_blocks = gathered.reshape(block_count, BLOCK, feature_count)
    xn = normalize(data_rows)
    mass_col = data_mass.reshape(local_rows, 1)
    links = block_links.astype(jnp.int32)
    scale_blocks = jnp.ones((block_count, BLOCK), jnp.float32)
    for sweep_index in range(ITERS - 1):
        _, part_total = sweep(xn, cn_blocks, scale_blocks, mass_col, links)
        whole_total = butterfly_sum(part_total, sizes)
        scale_blocks = mass_ratio * cand_mass.reshape(block_count, BLOCK) / whole_total
    ds_col, part_total, partial_sums = sweep(
        xn, cn_blocks, scale_blocks, mass_col, links, rows=data_rows
    )
    whole_total = butterfly_sum(part_total, sizes).reshape(-1)
    own_total = lax.dynamic_slice_in_dim(whole_total, own_start, local_cands)
    own_scale = mass_ratio * lax.dynamic_slice_in_dim(cand_mass, own_start, local_cands) / own_total
    flat_sums = partial_sums.reshape(cand_total, feature_count)
    share_rows = lax.psum_scatter(flat_sums, COL_AXES, scatter_dimension=0, tiled=True)
    own_sums = lax.psum(share_rows, ROW_AXES)
    new_support = own_sums / own_total[:, None]
    return (ds_col.reshape(local_rows), own_scale, new_support)


def solution(mesh):
    row_size, col_size = mesh.devices.shape
    fine = Mesh(mesh.devices.reshape(2, row_size // 4, 2, col_size // 2, 2), ALL_AXES)
    sizes = dict(fine.shape)
    placed = (
        P(ALL_AXES, None),
        P(ALL_AXES),
        P(ALL_AXES, None),
        P(COL_AXES, None),
        P(),
    )
    return jax.shard_map(
        functools.partial(on_device, sizes),
        mesh=fine,
        in_specs=placed,
        out_specs=(P(ALL_AXES), P(COL_AXES), P(COL_AXES, None)),
        check_vma=False,
    )
```

```python
import functools

import jax
import jax.numpy as jnp
from jax import lax
from jax.experimental import pallas as pl
from jax.experimental.pallas import tpu as pltpu
from jax.sharding import Mesh
from jax.sharding import PartitionSpec as P

BLOCK = 128
ITERS = 3


EPS = 0.05
OFFSET = 1.0

ROW_AXES = ("yh", "x", "c")
COL_AXES = ("z", "yl")
ALL_AXES = ROW_AXES + COL_AXES
TOTAL_GROUPS = (("yh", "c", "yl"), ("x",), ("z",))


def normalize(matrix):
    values = matrix.astype(jnp.float32)
    return (values * lax.rsqrt(jnp.mean(values * values, axis=1, keepdims=True) + 1e-06)).astype(
        jnp.bfloat16
    )


def butterfly_sum(x, axes, sizes):
    for axis in axes:
        n = sizes[axis]
        k = 1
        while k < n:
            x = x + lax.ppermute(x, axis, [(j, j ^ k) for j in range(n)])
            k *= 2
    return x


def group_sum(x, groups, sizes):
    for group in groups:
        n = 1
        for axis in group:
            n *= sizes[axis]
        me = lax.axis_index(group)
        held = [x] + [
            lax.ppermute(x, group, [(j, (j + k) % n) for j in range(n)]) for k in range(1, n)
        ]
        stacked = jnp.stack(held)
        ordered = jnp.take(stacked, (me - jnp.arange(n)) % n, axis=0)
        x = ordered[0]
        for i in range(1, n):
            x = x + ordered[i]
    return x


def _kernel_slot(xn, cn_ref, blk, inv_width, inv_count):
    cand = cn_ref[blk]
    scores = lax.dot_general(
        xn, cand, (((1,), (1,)), ((), ())), preferred_element_type=jnp.float32
    )
    return jnp.exp(scores * inv_width - OFFSET) * inv_count


def sweep_body(nbr, inv_width, inv_count, bary, links_ref, xn_ref, cn_ref, scale_ref, mass_ref,
               *rest):
    if bary:
        rows_ref, ds_ref, ct_ref, ws_ref, kbuf = rest
    else:
        ds_ref, ct_ref, kbuf = rest
    b = pl.program_id(0)

    @pl.when(b == 0)
    def _():
        ct_ref[...] = jnp.zeros_like(ct_ref)
        if bary:
            ws_ref[...] = jnp.zeros_like(ws_ref)

    xn = xn_ref[...]
    acc = jnp.zeros((BLOCK, BLOCK), jnp.float32)
    for s in range(nbr):
        blk = links_ref[b, s]
        k = _kernel_slot(xn, cn_ref, blk, inv_width, inv_count)
        kbuf[s] = k
        acc = acc + k * scale_ref[pl.ds(blk, 1), :]
    row_total = jnp.sum(acc, axis=1, keepdims=True)
    ds = mass_ref[...] / row_total
    ds_ref[...] = ds
    if bary:
        rows = rows_ref[...]
    for s in range(nbr):
        blk = links_ref[b, s]
        k = kbuf[s]
        part = jnp.sum(k * ds, axis=0, keepdims=True)
        ct_ref[pl.ds(blk, 1), :] += part
        if bary:
            w = (k * ds).astype(jnp.bfloat16)
            ws_ref[blk] += lax.dot_general(
                w, rows, (((0,), (0,)), ((), ())), preferred_element_type=jnp.float32
            )


def sweep(xn, cn_blocks, scale_blocks, mass_col, links, rows=None):
    local_rows, feature_count = xn.shape
    block_count = cn_blocks.shape[0]
    local_blocks, nbr = links.shape
    bary = rows is not None
    inv_width = 1.0 / (feature_count * EPS)
    inv_count = 1.0 / (nbr * BLOCK)
    in_specs = [
        pl.BlockSpec((BLOCK, feature_count), lambda b, L: (b, 0)),
        pl.BlockSpec((block_count, BLOCK, feature_count), lambda b, L: (0, 0, 0)),
        pl.BlockSpec((block_count, BLOCK), lambda b, L: (0, 0)),
        pl.BlockSpec((BLOCK, 1), lambda b, L: (b, 0)),
    ]
    out_specs = [
        pl.BlockSpec((BLOCK, 1), lambda b, L: (b, 0)),
        pl.BlockSpec((block_count, BLOCK), lambda b, L: (0, 0)),
    ]
    out_shape = [
        jax.ShapeDtypeStruct((local_rows, 1), jnp.float32),
        jax.ShapeDtypeStruct((block_count, BLOCK), jnp.float32),
    ]
    args = [links, xn, cn_blocks, scale_blocks, mass_col]
    if bary:
        in_specs.append(pl.BlockSpec((BLOCK, feature_count), lambda b, L: (b, 0)))
        out_specs.append(
            pl.BlockSpec((block_count, BLOCK, feature_count), lambda b, L: (0, 0, 0))
        )
        out_shape.append(jax.ShapeDtypeStruct((block_count, BLOCK, feature_count), jnp.float32))
        args.append(rows)
    flops = 2 * local_rows * nbr * BLOCK * feature_count * (2 if bary else 1)
    return pl.pallas_call(
        functools.partial(sweep_body, nbr, inv_width, inv_count, bary),
        grid_spec=pltpu.PrefetchScalarGridSpec(
            num_scalar_prefetch=1,
            grid=(local_blocks,),
            in_specs=in_specs,
            out_specs=out_specs,
            scratch_shapes=[pltpu.VMEM((nbr, BLOCK, BLOCK), jnp.float32)],
        ),
        out_shape=out_shape,
        compiler_params=pltpu.CompilerParams(
            dimension_semantics=("arbitrary",), vmem_limit_bytes=48 * 1024 * 1024
        ),
        cost_estimate=pl.CostEstimate(
            flops=flops,
            transcendentals=local_rows * nbr * BLOCK,
            bytes_accessed=block_count * BLOCK * feature_count * (2 + (4 if bary else 0))
            + local_rows * feature_count * (4 if bary else 2),
        ),
    )(*args)


def on_device(sizes, data_rows, data_mass, block_links, cand_rows, cand_mass):
    local_rows, feature_count = data_rows.shape
    local_cands = cand_rows.shape[0]
    row_devices = sizes["yh"] * sizes["x"] * sizes["c"]
    col_devices = sizes["z"] * sizes["yl"]
    cand_total = local_cands * col_devices
    block_count = cand_total // BLOCK
    mass_ratio = local_rows * row_devices / local_cands
    col_index = lax.axis_index("z") * sizes["yl"] + lax.axis_index("yl")
    own_start = col_index * local_cands
    gathered = lax.all_gather(
        lax.all_gather(normalize(cand_rows), "yl", axis=0, tiled=True), "z", axis=0, tiled=True
    )
    cn_blocks = gathered.reshape(block_count, BLOCK, feature_count)
    xn = normalize(data_rows)
    mass_col = data_mass.reshape(local_rows, 1)
    links = block_links.astype(jnp.int32)
    scale_blocks = jnp.ones((block_count, BLOCK), jnp.float32)
    for sweep_index in range(ITERS - 1):
        _, part_total = sweep(xn, cn_blocks, scale_blocks, mass_col, links)
        whole_total = group_sum(part_total, TOTAL_GROUPS, sizes)
        scale_blocks = mass_ratio * cand_mass.reshape(block_count, BLOCK) / whole_total
    ds_col, part_total, partial_sums = sweep(
        xn, cn_blocks, scale_blocks, mass_col, links, rows=data_rows
    )
    whole_total = group_sum(part_total, TOTAL_GROUPS, sizes).reshape(-1)
    own_total = lax.dynamic_slice_in_dim(whole_total, own_start, local_cands)
    own_scale = mass_ratio * lax.dynamic_slice_in_dim(cand_mass, own_start, local_cands) / own_total
    flat_sums = partial_sums.reshape(cand_total, feature_count)
    share_rows = lax.psum_scatter(flat_sums, COL_AXES, scatter_dimension=0, tiled=True)
    own_sums = butterfly_sum(share_rows, ("c", "x", "yh"), sizes)
    new_support = own_sums / own_total[:, None]
    return (ds_col.reshape(local_rows), own_scale, new_support)


def solution(mesh):
    row_size, col_size = mesh.devices.shape
    fine = Mesh(mesh.devices.reshape(2, row_size // 4, 2, col_size // 2, 2), ALL_AXES)
    sizes = dict(fine.shape)
    placed = (
        P(ALL_AXES, None),
        P(ALL_AXES),
        P(ALL_AXES, None),
        P(COL_AXES, None),
        P(),
    )
    return jax.shard_map(
        functools.partial(on_device, sizes),
        mesh=fine,
        in_specs=placed,
        out_specs=(P(ALL_AXES), P(COL_AXES), P(COL_AXES, None)),
        check_vma=False,
    )
```

```python
import functools

import jax
import jax.numpy as jnp
from jax import lax
from jax.experimental import pallas as pl
from jax.experimental.pallas import tpu as pltpu
from jax.sharding import Mesh
from jax.sharding import PartitionSpec as P

BLOCK = 128
ITERS = 3


EPS = 0.05
OFFSET = 1.0

ROW_AXES = ("yh", "x", "c")
COL_AXES = ("z", "yl")
ALL_AXES = ROW_AXES + COL_AXES
TOTAL_ORDER = ("c", "yl", "yh", "x", "z")


def normalize(matrix):
    values = matrix.astype(jnp.float32)
    return (values * lax.rsqrt(jnp.mean(values * values, axis=1, keepdims=True) + 1e-06)).astype(
        jnp.bfloat16
    )


def butterfly_sum(x, axes, sizes):
    for axis in axes:
        n = sizes[axis]
        k = 1
        while k < n:
            x = x + lax.ppermute(x, axis, [(j, j ^ k) for j in range(n)])
            k *= 2
    return x


def _kernel_slot(xn, cn_ref, blk, inv_width, inv_count):
    cand = cn_ref[blk]
    scores = lax.dot_general(
        xn, cand, (((1,), (1,)), ((), ())), preferred_element_type=jnp.float32
    )
    return jnp.exp(scores * inv_width - OFFSET) * inv_count


def sweep_body(nbr, inv_width, inv_count, bary, links_ref, xn_ref, cn_ref, scale_ref, mass_ref,
               *rest):
    if bary:
        rows_ref, ds_ref, ct_ref, ws_ref, kbuf = rest
    else:
        ds_ref, ct_ref, kbuf = rest
    b = pl.program_id(0)

    @pl.when(b == 0)
    def _():
        ct_ref[...] = jnp.zeros_like(ct_ref)
        if bary:
            ws_ref[...] = jnp.zeros_like(ws_ref)

    xn = xn_ref[...]
    acc = jnp.zeros((BLOCK, BLOCK), jnp.float32)
    for s in range(nbr):
        blk = links_ref[b, s]
        k = _kernel_slot(xn, cn_ref, blk, inv_width, inv_count)
        kbuf[s] = k
        acc = acc + k * scale_ref[pl.ds(blk, 1), :]
    row_total = jnp.sum(acc, axis=1, keepdims=True)
    ds = mass_ref[...] / row_total
    ds_ref[...] = ds
    if bary:
        rows = rows_ref[...]
    for s in range(nbr):
        blk = links_ref[b, s]
        k = kbuf[s]
        part = jnp.sum(k * ds, axis=0, keepdims=True)
        ct_ref[pl.ds(blk, 1), :] += part
        if bary:
            w = (k * ds).astype(jnp.bfloat16)
            ws_ref[blk] += lax.dot_general(
                w, rows, (((0,), (0,)), ((), ())), preferred_element_type=jnp.float32
            )


def sweep(xn, cn_blocks, scale_blocks, mass_col, links, rows=None):
    local_rows, feature_count = xn.shape
    block_count = cn_blocks.shape[0]
    local_blocks, nbr = links.shape
    bary = rows is not None
    inv_width = 1.0 / (feature_count * EPS)
    inv_count = 1.0 / (nbr * BLOCK)
    in_specs = [
        pl.BlockSpec((BLOCK, feature_count), lambda b, L: (b, 0)),
        pl.BlockSpec((block_count, BLOCK, feature_count), lambda b, L: (0, 0, 0)),
        pl.BlockSpec((block_count, BLOCK), lambda b, L: (0, 0)),
        pl.BlockSpec((BLOCK, 1), lambda b, L: (b, 0)),
    ]
    out_specs = [
        pl.BlockSpec((BLOCK, 1), lambda b, L: (b, 0)),
        pl.BlockSpec((block_count, BLOCK), lambda b, L: (0, 0)),
    ]
    out_shape = [
        jax.ShapeDtypeStruct((local_rows, 1), jnp.float32),
        jax.ShapeDtypeStruct((block_count, BLOCK), jnp.float32),
    ]
    args = [links, xn, cn_blocks, scale_blocks, mass_col]
    if bary:
        in_specs.append(pl.BlockSpec((BLOCK, feature_count), lambda b, L: (b, 0)))
        out_specs.append(
            pl.BlockSpec((block_count, BLOCK, feature_count), lambda b, L: (0, 0, 0))
        )
        out_shape.append(jax.ShapeDtypeStruct((block_count, BLOCK, feature_count), jnp.float32))
        args.append(rows)
    flops = 2 * local_rows * nbr * BLOCK * feature_count * (2 if bary else 1)
    return pl.pallas_call(
        functools.partial(sweep_body, nbr, inv_width, inv_count, bary),
        grid_spec=pltpu.PrefetchScalarGridSpec(
            num_scalar_prefetch=1,
            grid=(local_blocks,),
            in_specs=in_specs,
            out_specs=out_specs,
            scratch_shapes=[pltpu.VMEM((nbr, BLOCK, BLOCK), jnp.float32)],
        ),
        out_shape=out_shape,
        compiler_params=pltpu.CompilerParams(
            dimension_semantics=("arbitrary",), vmem_limit_bytes=48 * 1024 * 1024
        ),
        cost_estimate=pl.CostEstimate(
            flops=flops,
            transcendentals=local_rows * nbr * BLOCK,
            bytes_accessed=block_count * BLOCK * feature_count * (2 + (4 if bary else 0))
            + local_rows * feature_count * (4 if bary else 2),
        ),
    )(*args)


def on_device(sizes, data_rows, data_mass, block_links, cand_rows, cand_mass):
    local_rows, feature_count = data_rows.shape
    local_cands = cand_rows.shape[0]
    row_devices = sizes["yh"] * sizes["x"] * sizes["c"]
    col_devices = sizes["z"] * sizes["yl"]
    cand_total = local_cands * col_devices
    block_count = cand_total // BLOCK
    mass_ratio = local_rows * row_devices / local_cands
    col_index = lax.axis_index("z") * sizes["yl"] + lax.axis_index("yl")
    own_start = col_index * local_cands
    gathered = lax.all_gather(
        lax.all_gather(normalize(cand_rows), "yl", axis=0, tiled=True), "z", axis=0, tiled=True
    )
    cn_blocks = gathered.reshape(block_count, BLOCK, feature_count)
    xn = normalize(data_rows)
    mass_col = data_mass.reshape(local_rows, 1)
    links = block_links.astype(jnp.int32)
    scale_blocks = jnp.ones((block_count, BLOCK), jnp.float32)
    for sweep_index in range(ITERS - 1):
        _, part_total = sweep(xn, cn_blocks, scale_blocks, mass_col, links)
        whole_total = butterfly_sum(part_total, TOTAL_ORDER, sizes)
        scale_blocks = mass_ratio * cand_mass.reshape(block_count, BLOCK) / whole_total
    ds_col, part_total, partial_sums = sweep(
        xn, cn_blocks, scale_blocks, mass_col, links, rows=data_rows
    )
    whole_total = butterfly_sum(part_total, TOTAL_ORDER, sizes).reshape(-1)
    own_total = lax.dynamic_slice_in_dim(whole_total, own_start, local_cands)
    own_scale = mass_ratio * lax.dynamic_slice_in_dim(cand_mass, own_start, local_cands) / own_total
    flat_sums = partial_sums.reshape(cand_total, feature_count)
    share_rows = lax.psum_scatter(flat_sums, COL_AXES, scatter_dimension=0, tiled=True)
    own_sums = butterfly_sum(share_rows, ("c", "x", "yh"), sizes)
    new_support = own_sums / own_total[:, None]
    return (ds_col.reshape(local_rows), own_scale, new_support)


def solution(mesh):
    row_size, col_size = mesh.devices.shape
    fine = Mesh(mesh.devices.reshape(2, row_size // 4, 2, col_size // 2, 2), ALL_AXES)
    sizes = dict(fine.shape)
    placed = (
        P(ALL_AXES, None),
        P(ALL_AXES),
        P(ALL_AXES, None),
        P(COL_AXES, None),
        P(),
    )
    return jax.shard_map(
        functools.partial(on_device, sizes),
        mesh=fine,
        in_specs=placed,
        out_specs=(P(ALL_AXES), P(COL_AXES), P(COL_AXES, None)),
        check_vma=False,
    )
```

```python
import functools

import jax
import jax.numpy as jnp
from jax import lax
from jax.experimental import pallas as pl
from jax.experimental.pallas import tpu as pltpu
from jax.sharding import Mesh
from jax.sharding import PartitionSpec as P

BLOCK = 128
ITERS = 3


EPS = 0.05
OFFSET = 1.0

ROW_AXES = ("yh", "x", "c")
COL_AXES = ("z", "yl")
ALL_AXES = ROW_AXES + COL_AXES
TOTAL_ORDER = ("c", "yl", "yh", "x", "z")


def normalize(matrix):
    values = matrix.astype(jnp.float32)
    return (values * lax.rsqrt(jnp.mean(values * values, axis=1, keepdims=True) + 1e-06)).astype(
        jnp.bfloat16
    )


def butterfly_sum(x, axes, sizes):
    for axis in axes:
        n = sizes[axis]
        k = 1
        while k < n:
            x = x + lax.ppermute(x, axis, [(j, j ^ k) for j in range(n)])
            k *= 2
    return x


def _kernel_slot(xn, cn_ref, blk, inv_width, inv_count):
    cand = cn_ref[blk]
    scores = lax.dot_general(
        xn, cand, (((1,), (1,)), ((), ())), preferred_element_type=jnp.float32
    )
    return jnp.exp(scores * inv_width - OFFSET) * inv_count


def sweep_body(nbr, inv_width, inv_count, bary, links_ref, xn_ref, cn_ref, scale_ref, mass_ref,
               *rest):
    if bary:
        rows_ref, ds_ref, ct_ref, ws_ref, kbuf = rest
    else:
        ds_ref, ct_ref, kbuf = rest
    b = pl.program_id(0)

    @pl.when(b == 0)
    def _():
        ct_ref[...] = jnp.zeros_like(ct_ref)
        if bary:
            ws_ref[...] = jnp.zeros_like(ws_ref)

    xn = xn_ref[...]
    acc = jnp.zeros((BLOCK, BLOCK), jnp.float32)
    for s in range(nbr):
        blk = links_ref[b, s]
        k = _kernel_slot(xn, cn_ref, blk, inv_width, inv_count)
        kbuf[s] = k
        acc = acc + k * scale_ref[pl.ds(blk, 1), :]
    row_total = jnp.sum(acc, axis=1, keepdims=True)
    ds = mass_ref[...] / row_total
    ds_ref[...] = ds
    if bary:
        rows = rows_ref[...]
    for s in range(nbr):
        blk = links_ref[b, s]
        k = kbuf[s]
        part = jnp.sum(k * ds, axis=0, keepdims=True)
        ct_ref[pl.ds(blk, 1), :] += part
        if bary:
            w = (k * ds).astype(jnp.bfloat16)
            ws_ref[blk] += lax.dot_general(
                w, rows, (((0,), (0,)), ((), ())), preferred_element_type=jnp.float32
            )


def sweep(xn, cn_blocks, scale_blocks, mass_col, links, rows=None):
    local_rows, feature_count = xn.shape
    block_count = cn_blocks.shape[0]
    local_blocks, nbr = links.shape
    bary = rows is not None
    inv_width = 1.0 / (feature_count * EPS)
    inv_count = 1.0 / (nbr * BLOCK)
    in_specs = [
        pl.BlockSpec((BLOCK, feature_count), lambda b, L: (b, 0)),
        pl.BlockSpec((block_count, BLOCK, feature_count), lambda b, L: (0, 0, 0)),
        pl.BlockSpec((block_count, BLOCK), lambda b, L: (0, 0)),
        pl.BlockSpec((BLOCK, 1), lambda b, L: (b, 0)),
    ]
    out_specs = [
        pl.BlockSpec((BLOCK, 1), lambda b, L: (b, 0)),
        pl.BlockSpec((block_count, BLOCK), lambda b, L: (0, 0)),
    ]
    out_shape = [
        jax.ShapeDtypeStruct((local_rows, 1), jnp.float32),
        jax.ShapeDtypeStruct((block_count, BLOCK), jnp.float32),
    ]
    args = [links, xn, cn_blocks, scale_blocks, mass_col]
    if bary:
        in_specs.append(pl.BlockSpec((BLOCK, feature_count), lambda b, L: (b, 0)))
        out_specs.append(
            pl.BlockSpec((block_count, BLOCK, feature_count), lambda b, L: (0, 0, 0))
        )
        out_shape.append(jax.ShapeDtypeStruct((block_count, BLOCK, feature_count), jnp.float32))
        args.append(rows)
    flops = 2 * local_rows * nbr * BLOCK * feature_count * (2 if bary else 1)
    return pl.pallas_call(
        functools.partial(sweep_body, nbr, inv_width, inv_count, bary),
        grid_spec=pltpu.PrefetchScalarGridSpec(
            num_scalar_prefetch=1,
            grid=(local_blocks,),
            in_specs=in_specs,
            out_specs=out_specs,
            scratch_shapes=[pltpu.VMEM((nbr, BLOCK, BLOCK), jnp.float32)],
        ),
        out_shape=out_shape,
        compiler_params=pltpu.CompilerParams(
            dimension_semantics=("arbitrary",), vmem_limit_bytes=48 * 1024 * 1024
        ),
        cost_estimate=pl.CostEstimate(
            flops=flops,
            transcendentals=local_rows * nbr * BLOCK,
            bytes_accessed=block_count * BLOCK * feature_count * (2 + (4 if bary else 0))
            + local_rows * feature_count * (4 if bary else 2),
        ),
    )(*args)


def on_device(sizes, data_rows, data_mass, block_links, cand_rows, cand_mass):
    local_rows, feature_count = data_rows.shape
    local_cands = cand_rows.shape[0]
    row_devices = sizes["yh"] * sizes["x"] * sizes["c"]
    col_devices = sizes["z"] * sizes["yl"]
    cand_total = local_cands * col_devices
    block_count = cand_total // BLOCK
    mass_ratio = local_rows * row_devices / local_cands
    col_index = lax.axis_index("z") * sizes["yl"] + lax.axis_index("yl")
    own_start = col_index * local_cands
    gathered = lax.all_gather(
        lax.all_gather(normalize(cand_rows), "yl", axis=0, tiled=True), "z", axis=0, tiled=True
    )
    cn_blocks = gathered.reshape(block_count, BLOCK, feature_count)
    xn = normalize(data_rows)
    mass_col = data_mass.reshape(local_rows, 1)
    links = block_links.astype(jnp.int32)
    scale_blocks = jnp.ones((block_count, BLOCK), jnp.float32)
    for sweep_index in range(ITERS - 1):
        _, part_total = sweep(xn, cn_blocks, scale_blocks, mass_col, links)
        whole_total = butterfly_sum(part_total, TOTAL_ORDER, sizes)
        scale_blocks = mass_ratio * cand_mass.reshape(block_count, BLOCK) / whole_total
    ds_col, part_total, partial_sums = sweep(
        xn, cn_blocks, scale_blocks, mass_col, links, rows=data_rows
    )
    pad = 8
    totals = jnp.pad(part_total.reshape(col_devices, 1, local_cands), ((0, 0), (0, pad - 1), (0, 0)))
    packed = jnp.concatenate(
        [partial_sums.reshape(col_devices, local_cands, feature_count), totals], axis=1
    ).reshape(col_devices * (local_cands + pad), feature_count)
    joined = lax.psum_scatter(packed, COL_AXES, scatter_dimension=0, tiled=True)
    joined = butterfly_sum(joined, ("c", "x", "yh"), sizes)
    own_sums = joined[:local_cands]
    own_total = joined[local_cands]
    own_scale = mass_ratio * lax.dynamic_slice_in_dim(cand_mass, own_start, local_cands) / own_total
    new_support = own_sums / own_total[:, None]
    return (ds_col.reshape(local_rows), own_scale, new_support)


def solution(mesh):
    row_size, col_size = mesh.devices.shape
    fine = Mesh(mesh.devices.reshape(2, row_size // 4, 2, col_size // 2, 2), ALL_AXES)
    sizes = dict(fine.shape)
    placed = (
        P(ALL_AXES, None),
        P(ALL_AXES),
        P(ALL_AXES, None),
        P(COL_AXES, None),
        P(),
    )
    return jax.shard_map(
        functools.partial(on_device, sizes),
        mesh=fine,
        in_specs=placed,
        out_specs=(P(ALL_AXES), P(COL_AXES), P(COL_AXES, None)),
        check_vma=False,
    )
```

```python
import functools

import jax
import jax.numpy as jnp
from jax import lax
from jax.experimental import pallas as pl
from jax.experimental.pallas import tpu as pltpu
from jax.sharding import Mesh
from jax.sharding import PartitionSpec as P

BLOCK = 128
ITERS = 3


EPS = 0.05
OFFSET = 1.0
PAD = 8

ROW_AXES = ("yh", "x", "c")
COL_AXES = ("z", "yl")
ALL_AXES = ROW_AXES + COL_AXES
TOTAL_ORDER = ("c", "yl", "yh", "x", "z")


def normalize(matrix):
    values = matrix.astype(jnp.float32)
    return (values * lax.rsqrt(jnp.mean(values * values, axis=1, keepdims=True) + 1e-06)).astype(
        jnp.bfloat16
    )


def butterfly_sum(x, axes, sizes):
    for axis in axes:
        n = sizes[axis]
        k = 1
        while k < n:
            x = x + lax.ppermute(x, axis, [(j, j ^ k) for j in range(n)])
            k *= 2
    return x


def _kernel_slot(xn, cn_ref, blk, inv_width, inv_count):
    cand = cn_ref[blk]
    scores = lax.dot_general(
        xn, cand, (((1,), (1,)), ((), ())), preferred_element_type=jnp.float32
    )
    return jnp.exp(scores * inv_width - OFFSET) * inv_count


def sweep_body(nbr, inv_width, inv_count, bary, links_ref, xn_ref, cn_ref, scale_ref, mass_ref,
               *rest):
    if bary:
        rows_ref, ds_ref, ws_ref, kbuf = rest
    else:
        ds_ref, ct_ref, kbuf = rest
    b = pl.program_id(0)

    @pl.when(b == 0)
    def _():
        if bary:
            ws_ref[...] = jnp.zeros_like(ws_ref)
        else:
            ct_ref[...] = jnp.zeros_like(ct_ref)

    xn = xn_ref[...]
    acc = jnp.zeros((BLOCK, BLOCK), jnp.float32)
    for s in range(nbr):
        blk = links_ref[b, s]
        k = _kernel_slot(xn, cn_ref, blk, inv_width, inv_count)
        kbuf[s] = k
        acc = acc + k * scale_ref[pl.ds(blk, 1), :]
    row_total = jnp.sum(acc, axis=1, keepdims=True)
    ds = mass_ref[...] / row_total
    ds_ref[...] = ds
    if bary:
        rows = rows_ref[...]
    for s in range(nbr):
        blk = links_ref[b, s]
        k = kbuf[s]
        part = jnp.sum(k * ds, axis=0, keepdims=True)
        if bary:
            q = blk // 2
            half = pl.multiple_of((blk % 2) * BLOCK, BLOCK)
            ws_ref[q, pl.ds(2 * BLOCK, 1), pl.ds(half, BLOCK)] += part
            w = (k * ds).astype(jnp.bfloat16)
            ws_ref[q, pl.ds(half, BLOCK), :] += lax.dot_general(
                w, rows, (((0,), (0,)), ((), ())), preferred_element_type=jnp.float32
            )
        else:
            ct_ref[pl.ds(blk, 1), :] += part


def sweep(xn, cn_blocks, scale_blocks, mass_col, links, rows=None):
    local_rows, feature_count = xn.shape
    block_count = cn_blocks.shape[0]
    local_blocks, nbr = links.shape
    bary = rows is not None
    inv_width = 1.0 / (feature_count * EPS)
    inv_count = 1.0 / (nbr * BLOCK)
    in_specs = [
        pl.BlockSpec((BLOCK, feature_count), lambda b, L: (b, 0)),
        pl.BlockSpec((block_count, BLOCK, feature_count), lambda b, L: (0, 0, 0)),
        pl.BlockSpec((block_count, BLOCK), lambda b, L: (0, 0)),
        pl.BlockSpec((BLOCK, 1), lambda b, L: (b, 0)),
    ]
    out_specs = [pl.BlockSpec((BLOCK, 1), lambda b, L: (b, 0))]
    out_shape = [jax.ShapeDtypeStruct((local_rows, 1), jnp.float32)]
    packed_rows = 2 * BLOCK + PAD
    args = [links, xn, cn_blocks, scale_blocks, mass_col]
    if bary:
        in_specs.append(pl.BlockSpec((BLOCK, feature_count), lambda b, L: (b, 0)))
        packed = (block_count // 2, packed_rows, feature_count)
        out_specs.append(pl.BlockSpec(packed, lambda b, L: (0, 0, 0)))
        out_shape.append(jax.ShapeDtypeStruct(packed, jnp.float32))
        args.append(rows)
    else:
        out_specs.append(pl.BlockSpec((block_count, BLOCK), lambda b, L: (0, 0)))
        out_shape.append(jax.ShapeDtypeStruct((block_count, BLOCK), jnp.float32))
    flops = 2 * local_rows * nbr * BLOCK * feature_count * (2 if bary else 1)
    return pl.pallas_call(
        functools.partial(sweep_body, nbr, inv_width, inv_count, bary),
        grid_spec=pltpu.PrefetchScalarGridSpec(
            num_scalar_prefetch=1,
            grid=(local_blocks,),
            in_specs=in_specs,
            out_specs=out_specs,
            scratch_shapes=[pltpu.VMEM((nbr, BLOCK, BLOCK), jnp.float32)],
        ),
        out_shape=out_shape,
        compiler_params=pltpu.CompilerParams(
            dimension_semantics=("arbitrary",), vmem_limit_bytes=48 * 1024 * 1024
        ),
        cost_estimate=pl.CostEstimate(
            flops=flops,
            transcendentals=local_rows * nbr * BLOCK,
            bytes_accessed=block_count * BLOCK * feature_count * (2 + (4 if bary else 0))
            + local_rows * feature_count * (4 if bary else 2),
        ),
    )(*args)


def on_device(sizes, data_rows, data_mass, block_links, cand_rows, cand_mass):
    local_rows, feature_count = data_rows.shape
    local_cands = cand_rows.shape[0]
    row_devices = sizes["yh"] * sizes["x"] * sizes["c"]
    col_devices = sizes["z"] * sizes["yl"]
    cand_total = local_cands * col_devices
    block_count = cand_total // BLOCK
    mass_ratio = local_rows * row_devices / local_cands
    col_index = lax.axis_index("z") * sizes["yl"] + lax.axis_index("yl")
    own_start = col_index * local_cands
    gathered = lax.all_gather(
        lax.all_gather(normalize(cand_rows), "yl", axis=0, tiled=True), "z", axis=0, tiled=True
    )
    cn_blocks = gathered.reshape(block_count, BLOCK, feature_count)
    xn = normalize(data_rows)
    mass_col = data_mass.reshape(local_rows, 1)
    links = block_links.astype(jnp.int32)
    scale_blocks = jnp.ones((block_count, BLOCK), jnp.float32)
    for sweep_index in range(ITERS - 1):
        _, part_total = sweep(xn, cn_blocks, scale_blocks, mass_col, links)
        whole_total = butterfly_sum(part_total, TOTAL_ORDER, sizes)
        scale_blocks = mass_ratio * cand_mass.reshape(block_count, BLOCK) / whole_total
    ds_col, packed = sweep(xn, cn_blocks, scale_blocks, mass_col, links, rows=data_rows)
    joined = lax.psum_scatter(packed.reshape(-1, feature_count), COL_AXES, scatter_dimension=0, tiled=True)
    joined = butterfly_sum(joined, ("c", "x", "yh"), sizes)
    own_sums = joined[:local_cands]
    own_total = joined[local_cands]
    own_scale = mass_ratio * lax.dynamic_slice_in_dim(cand_mass, own_start, local_cands) / own_total
    new_support = own_sums / own_total[:, None]
    return (ds_col.reshape(local_rows), own_scale, new_support)


def solution(mesh):
    row_size, col_size = mesh.devices.shape
    fine = Mesh(mesh.devices.reshape(2, row_size // 4, 2, col_size // 2, 2), ALL_AXES)
    sizes = dict(fine.shape)
    placed = (
        P(ALL_AXES, None),
        P(ALL_AXES),
        P(ALL_AXES, None),
        P(COL_AXES, None),
        P(),
    )
    return jax.shard_map(
        functools.partial(on_device, sizes),
        mesh=fine,
        in_specs=placed,
        out_specs=(P(ALL_AXES), P(COL_AXES), P(COL_AXES, None)),
        check_vma=False,
    )
```

```python
import functools

import jax
import jax.numpy as jnp
from jax import lax
from jax.experimental import pallas as pl
from jax.experimental.pallas import tpu as pltpu
from jax.sharding import Mesh
from jax.sharding import PartitionSpec as P

BLOCK = 128
ITERS = 3


EPS = 0.05
OFFSET = 1.0
PAD = 8

ROW_AXES = ("yh", "x", "c")
COL_AXES = ("z", "yl")
ALL_AXES = ROW_AXES + COL_AXES
TOTAL_ORDER = ("c", "yl", "yh", "x", "z")


def normalize(matrix):
    values = matrix.astype(jnp.float32)
    return (values * lax.rsqrt(jnp.mean(values * values, axis=1, keepdims=True) + 1e-06)).astype(
        jnp.bfloat16
    )


def butterfly_sum(x, axes, sizes):
    for axis in axes:
        n = sizes[axis]
        k = 1
        while k < n:
            x = x + lax.ppermute(x, axis, [(j, j ^ k) for j in range(n)])
            k *= 2
    return x


def _kernel_slot(xn, cn_ref, blk, inv_width, inv_count):
    cand = cn_ref[blk]
    scores = lax.dot_general(
        xn, cand, (((1,), (1,)), ((), ())), preferred_element_type=jnp.float32
    )
    return jnp.exp(scores * inv_width - OFFSET) * inv_count


def sweep_body(nbr, inv_width, inv_count, bary, first, links_ref, *refs):
    if first:
        xn_ref, cn_ref, scale_ref, mass_ref, ds_ref, ct_ref, kbuf = refs
    elif bary:
        kbuf, scale_ref, mass_ref, rows_ref, ds_ref, ws_ref = refs
    else:
        kbuf, scale_ref, mass_ref, ds_ref, ct_ref = refs
    b = pl.program_id(0)

    @pl.when(b == 0)
    def _():
        if bary:
            ws_ref[...] = jnp.zeros_like(ws_ref)
        else:
            ct_ref[...] = jnp.zeros_like(ct_ref)

    acc = jnp.zeros((BLOCK, BLOCK), jnp.float32)
    if first:
        xn = xn_ref[...]
    for s in range(nbr):
        blk = links_ref[b, s]
        if first:
            k = _kernel_slot(xn, cn_ref, blk, inv_width, inv_count)
            kbuf[s] = k
        else:
            k = kbuf[s]
        acc = acc + k * scale_ref[pl.ds(blk, 1), :]
    row_total = jnp.sum(acc, axis=1, keepdims=True)
    ds = mass_ref[...] / row_total
    ds_ref[...] = ds
    if bary:
        rows = rows_ref[...]
    for s in range(nbr):
        blk = links_ref[b, s]
        k = kbuf[s]
        part = jnp.sum(k * ds, axis=0, keepdims=True)
        if bary:
            q = blk // 2
            half = pl.multiple_of((blk % 2) * BLOCK, BLOCK)
            ws_ref[q, pl.ds(2 * BLOCK, 1), pl.ds(half, BLOCK)] += part
            w = (k * ds).astype(jnp.bfloat16)
            ws_ref[q, pl.ds(half, BLOCK), :] += lax.dot_general(
                w, rows, (((0,), (0,)), ((), ())), preferred_element_type=jnp.float32
            )
        else:
            ct_ref[pl.ds(blk, 1), :] += part


def sweep(links, scale_blocks, mass_col, xn=None, cn_blocks=None, kern=None, rows=None):
    local_blocks, nbr = links.shape
    local_rows = local_blocks * BLOCK
    block_count = scale_blocks.shape[0]
    feature_count = 256 if rows is None else rows.shape[1]
    first = kern is None
    bary = rows is not None
    k_spec = pl.BlockSpec((nbr, BLOCK, BLOCK), lambda b, L: (b, 0, 0))
    k_shape = jax.ShapeDtypeStruct((local_blocks * nbr, BLOCK, BLOCK), jnp.float32)
    small = [
        pl.BlockSpec((block_count, BLOCK), lambda b, L: (0, 0)),
        pl.BlockSpec((BLOCK, 1), lambda b, L: (b, 0)),
    ]
    out_specs = [pl.BlockSpec((BLOCK, 1), lambda b, L: (b, 0))]
    out_shape = [jax.ShapeDtypeStruct((local_rows, 1), jnp.float32)]
    ct_spec = pl.BlockSpec((block_count, BLOCK), lambda b, L: (0, 0))
    ct_shape = jax.ShapeDtypeStruct((block_count, BLOCK), jnp.float32)
    flops = 6 * local_rows * nbr * BLOCK
    transcendentals = 0
    if first:
        feature_count = xn.shape[1]
        in_specs = [
            pl.BlockSpec((BLOCK, feature_count), lambda b, L: (b, 0)),
            pl.BlockSpec((block_count, BLOCK, feature_count), lambda b, L: (0, 0, 0)),
        ] + small
        args = [links, xn, cn_blocks, scale_blocks, mass_col]
        out_specs += [ct_spec, k_spec]
        out_shape += [ct_shape, k_shape]
        flops += 2 * local_rows * nbr * BLOCK * feature_count
        transcendentals = local_rows * nbr * BLOCK
    elif bary:
        packed_rows = 2 * BLOCK + PAD
        packed = (block_count // 2, packed_rows, feature_count)
        in_specs = [k_spec] + small + [pl.BlockSpec((BLOCK, feature_count), lambda b, L: (b, 0))]
        args = [links, kern, scale_blocks, mass_col, rows]
        out_specs.append(pl.BlockSpec(packed, lambda b, L: (0, 0, 0)))
        out_shape.append(jax.ShapeDtypeStruct(packed, jnp.float32))
        flops += 2 * local_rows * nbr * BLOCK * feature_count
    else:
        in_specs = [k_spec] + small
        args = [links, kern, scale_blocks, mass_col]
        out_specs.append(ct_spec)
        out_shape.append(ct_shape)
    inv_width = 1.0 / (feature_count * EPS)
    inv_count = 1.0 / (nbr * BLOCK)
    return pl.pallas_call(
        functools.partial(sweep_body, nbr, inv_width, inv_count, bary, first),
        grid_spec=pltpu.PrefetchScalarGridSpec(
            num_scalar_prefetch=1,
            grid=(local_blocks,),
            in_specs=in_specs,
            out_specs=out_specs,
        ),
        out_shape=out_shape,
        compiler_params=pltpu.CompilerParams(
            dimension_semantics=("arbitrary",), vmem_limit_bytes=48 * 1024 * 1024
        ),
        cost_estimate=pl.CostEstimate(
            flops=flops,
            transcendentals=transcendentals,
            bytes_accessed=local_rows * nbr * BLOCK * 4 + block_count * BLOCK * feature_count * 4,
        ),
    )(*args)


def on_device(sizes, data_rows, data_mass, block_links, cand_rows, cand_mass):
    local_rows, feature_count = data_rows.shape
    local_cands = cand_rows.shape[0]
    row_devices = sizes["yh"] * sizes["x"] * sizes["c"]
    col_devices = sizes["z"] * sizes["yl"]
    cand_total = local_cands * col_devices
    block_count = cand_total // BLOCK
    mass_ratio = local_rows * row_devices / local_cands
    col_index = lax.axis_index("z") * sizes["yl"] + lax.axis_index("yl")
    own_start = col_index * local_cands
    gathered = lax.all_gather(
        lax.all_gather(normalize(cand_rows), "yl", axis=0, tiled=True), "z", axis=0, tiled=True
    )
    cn_blocks = gathered.reshape(block_count, BLOCK, feature_count)
    xn = normalize(data_rows)
    mass_col = data_mass.reshape(local_rows, 1)
    links = block_links.astype(jnp.int32)
    scale_blocks = jnp.ones((block_count, BLOCK), jnp.float32)
    kern = None
    for sweep_index in range(ITERS - 1):
        if kern is None:
            _, part_total, kern = sweep(links, scale_blocks, mass_col, xn=xn, cn_blocks=cn_blocks)
        else:
            _, part_total = sweep(links, scale_blocks, mass_col, kern=kern)
        whole_total = butterfly_sum(part_total, TOTAL_ORDER, sizes)
        scale_blocks = mass_ratio * cand_mass.reshape(block_count, BLOCK) / whole_total
    ds_col, packed = sweep(links, scale_blocks, mass_col, kern=kern, rows=data_rows)
    joined = lax.psum_scatter(packed.reshape(-1, feature_count), COL_AXES, scatter_dimension=0, tiled=True)
    joined = butterfly_sum(joined, ("c", "x", "yh"), sizes)
    own_sums = joined[:local_cands]
    own_total = joined[local_cands]
    own_scale = mass_ratio * lax.dynamic_slice_in_dim(cand_mass, own_start, local_cands) / own_total
    new_support = own_sums / own_total[:, None]
    return (ds_col.reshape(local_rows), own_scale, new_support)


def solution(mesh):
    row_size, col_size = mesh.devices.shape
    fine = Mesh(mesh.devices.reshape(2, row_size // 4, 2, col_size // 2, 2), ALL_AXES)
    sizes = dict(fine.shape)
    placed = (
        P(ALL_AXES, None),
        P(ALL_AXES),
        P(ALL_AXES, None),
        P(COL_AXES, None),
        P(),
    )
    return jax.shard_map(
        functools.partial(on_device, sizes),
        mesh=fine,
        in_specs=placed,
        out_specs=(P(ALL_AXES), P(COL_AXES), P(COL_AXES, None)),
        check_vma=False,
    )
```

```python
import functools

import jax
import jax.numpy as jnp
from jax import lax
from jax.experimental import pallas as pl
from jax.experimental.pallas import tpu as pltpu
from jax.sharding import Mesh
from jax.sharding import PartitionSpec as P

BLOCK = 128
ITERS = 3


EPS = 0.05
OFFSET = 1.0
PAD = 8

ROW_AXES = ("yh", "x", "c")
COL_AXES = ("z", "yl")
ALL_AXES = ROW_AXES + COL_AXES
TOTAL_ORDER = ("c", "yl", "yh", "x", "z")


def normalize(matrix):
    values = matrix.astype(jnp.float32)
    return (values * lax.rsqrt(jnp.mean(values * values, axis=1, keepdims=True) + 1e-06)).astype(
        jnp.bfloat16
    )


def butterfly_sum(x, axes, sizes):
    for axis in axes:
        n = sizes[axis]
        k = 1
        while k < n:
            x = x + lax.ppermute(x, axis, [(j, j ^ k) for j in range(n)])
            k *= 2
    return x


def _kernel_slot(xn, cn_ref, blk, inv_width, inv_count):
    cand = cn_ref[blk]
    scores = lax.dot_general(
        xn, cand, (((1,), (1,)), ((), ())), preferred_element_type=jnp.float32
    )
    return jnp.exp(scores * inv_width - OFFSET) * inv_count


def sweep_body(nbr, inv_width, inv_count, bary, links_ref, xn_ref, cn_ref, scale_ref, mass_ref,
               *rest):
    if bary:
        rows_ref, ds_ref, ws_ref, kbuf = rest
    else:
        ds_ref, ct_ref, kbuf = rest
    b = pl.program_id(0)

    @pl.when(b == 0)
    def _():
        if bary:
            ws_ref[...] = jnp.zeros_like(ws_ref)
        else:
            ct_ref[...] = jnp.zeros_like(ct_ref)

    xn = xn_ref[...]
    acc = jnp.zeros((BLOCK, BLOCK), jnp.float32)
    for s in range(nbr):
        blk = links_ref[b, s]
        k = _kernel_slot(xn, cn_ref, blk, inv_width, inv_count)
        kbuf[s] = k
        acc = acc + k * scale_ref[pl.ds(blk, 1), :]
    row_total = jnp.sum(acc, axis=1, keepdims=True)
    ds = mass_ref[...] / row_total
    ds_ref[...] = ds
    if bary:
        rows = rows_ref[...]
    for s in range(nbr):
        blk = links_ref[b, s]
        k = kbuf[s]
        part = jnp.sum(k * ds, axis=0, keepdims=True)
        if bary:
            half_count = ws_ref.shape[0] // 2
            slot = (blk % 2) * half_count + blk // 2
            ws_ref[slot, pl.ds(BLOCK, 1), pl.ds(0, BLOCK)] += part
            w = (k * ds).astype(jnp.bfloat16)
            ws_ref[slot, pl.ds(0, BLOCK), :] += lax.dot_general(
                w, rows, (((0,), (0,)), ((), ())), preferred_element_type=jnp.float32
            )
        else:
            ct_ref[pl.ds(blk, 1), :] += part


def sweep(xn, cn_blocks, scale_blocks, mass_col, links, rows=None):
    local_rows, feature_count = xn.shape
    block_count = cn_blocks.shape[0]
    local_blocks, nbr = links.shape
    bary = rows is not None
    inv_width = 1.0 / (feature_count * EPS)
    inv_count = 1.0 / (nbr * BLOCK)
    in_specs = [
        pl.BlockSpec((BLOCK, feature_count), lambda b, L: (b, 0)),
        pl.BlockSpec((block_count, BLOCK, feature_count), lambda b, L: (0, 0, 0)),
        pl.BlockSpec((block_count, BLOCK), lambda b, L: (0, 0)),
        pl.BlockSpec((BLOCK, 1), lambda b, L: (b, 0)),
    ]
    out_specs = [pl.BlockSpec((BLOCK, 1), lambda b, L: (b, 0))]
    out_shape = [jax.ShapeDtypeStruct((local_rows, 1), jnp.float32)]
    packed_rows = BLOCK + PAD
    args = [links, xn, cn_blocks, scale_blocks, mass_col]
    if bary:
        in_specs.append(pl.BlockSpec((BLOCK, feature_count), lambda b, L: (b, 0)))
        packed = (block_count, packed_rows, feature_count)
        out_specs.append(pl.BlockSpec(packed, lambda b, L: (0, 0, 0)))
        out_shape.append(jax.ShapeDtypeStruct(packed, jnp.float32))
        args.append(rows)
    else:
        out_specs.append(pl.BlockSpec((block_count, BLOCK), lambda b, L: (0, 0)))
        out_shape.append(jax.ShapeDtypeStruct((block_count, BLOCK), jnp.float32))
    flops = 2 * local_rows * nbr * BLOCK * feature_count * (2 if bary else 1)
    return pl.pallas_call(
        functools.partial(sweep_body, nbr, inv_width, inv_count, bary),
        grid_spec=pltpu.PrefetchScalarGridSpec(
            num_scalar_prefetch=1,
            grid=(local_blocks,),
            in_specs=in_specs,
            out_specs=out_specs,
            scratch_shapes=[pltpu.VMEM((nbr, BLOCK, BLOCK), jnp.float32)],
        ),
        out_shape=out_shape,
        compiler_params=pltpu.CompilerParams(
            dimension_semantics=("arbitrary",), vmem_limit_bytes=48 * 1024 * 1024
        ),
        cost_estimate=pl.CostEstimate(
            flops=flops,
            transcendentals=local_rows * nbr * BLOCK,
            bytes_accessed=block_count * BLOCK * feature_count * (2 + (4 if bary else 0))
            + local_rows * feature_count * (4 if bary else 2),
        ),
    )(*args)


def on_device(sizes, data_rows, data_mass, block_links, cand_rows, cand_mass):
    local_rows, feature_count = data_rows.shape
    local_cands = cand_rows.shape[0]
    row_devices = sizes["yh"] * sizes["x"] * sizes["c"]
    col_devices = sizes["z"] * sizes["yl"]
    cand_total = local_cands * col_devices
    block_count = cand_total // BLOCK
    mass_ratio = local_rows * row_devices / local_cands
    col_index = lax.axis_index("z") * sizes["yl"] + lax.axis_index("yl")
    own_start = col_index * local_cands
    gathered = lax.all_gather(
        lax.all_gather(normalize(cand_rows), "yl", axis=0, tiled=True), "z", axis=0, tiled=True
    )
    cn_blocks = gathered.reshape(block_count, BLOCK, feature_count)
    xn = normalize(data_rows)
    mass_col = data_mass.reshape(local_rows, 1)
    links = block_links.astype(jnp.int32)
    scale_blocks = jnp.ones((block_count, BLOCK), jnp.float32)
    for sweep_index in range(ITERS - 1):
        _, part_total = sweep(xn, cn_blocks, scale_blocks, mass_col, links)
        whole_total = butterfly_sum(part_total, TOTAL_ORDER, sizes)
        scale_blocks = mass_ratio * cand_mass.reshape(block_count, BLOCK) / whole_total
    ds_col, packed = sweep(xn, cn_blocks, scale_blocks, mass_col, links, rows=data_rows)
    joined = lax.psum_scatter(
        packed.reshape(-1, feature_count), ("c",) + COL_AXES, scatter_dimension=0, tiled=True
    )
    joined = butterfly_sum(joined, ("x", "yh"), sizes)
    other = lax.ppermute(joined, "c", [(0, 1), (1, 0)])
    first_core = lax.axis_index("c") == 0
    low = jnp.where(first_core, joined, other)
    high = jnp.where(first_core, other, joined)
    own_sums = jnp.concatenate([low[:BLOCK], high[:BLOCK]], axis=0)
    own_total = jnp.concatenate([low[BLOCK, :BLOCK], high[BLOCK, :BLOCK]], axis=0)
    own_scale = mass_ratio * lax.dynamic_slice_in_dim(cand_mass, own_start, local_cands) / own_total
    new_support = own_sums / own_total[:, None]
    return (ds_col.reshape(local_rows), own_scale, new_support)


def solution(mesh):
    row_size, col_size = mesh.devices.shape
    fine = Mesh(mesh.devices.reshape(2, row_size // 4, 2, col_size // 2, 2), ALL_AXES)
    sizes = dict(fine.shape)
    placed = (
        P(ALL_AXES, None),
        P(ALL_AXES),
        P(ALL_AXES, None),
        P(COL_AXES, None),
        P(),
    )
    return jax.shard_map(
        functools.partial(on_device, sizes),
        mesh=fine,
        in_specs=placed,
        out_specs=(P(ALL_AXES), P(COL_AXES), P(COL_AXES, None)),
        check_vma=False,
    )
```

```python
import functools
import math

import jax
import jax.numpy as jnp
from jax import lax
from jax.experimental import pallas as pl
from jax.experimental.pallas import tpu as pltpu
from jax.sharding import Mesh
from jax.sharding import PartitionSpec as P

BLOCK = 128
ITERS = 3


EPS = 0.05
OFFSET = 1.0
PAD = 8

ROW_AXES = ("yh", "x", "c")
COL_AXES = ("z", "yl")
ALL_AXES = ROW_AXES + COL_AXES
TOTAL_ORDER = ("c", "yl", "yh", "x", "z")


def normalize(matrix):
    values = matrix.astype(jnp.float32)
    return (values * lax.rsqrt(jnp.mean(values * values, axis=1, keepdims=True) + 1e-06)).astype(
        jnp.bfloat16
    )


def butterfly_sum(x, axes, sizes):
    for axis in axes:
        n = sizes[axis]
        k = 1
        while k < n:
            x = x + lax.ppermute(x, axis, [(j, j ^ k) for j in range(n)])
            k *= 2
    return x


def _kernel_slot(xn, cn_ref, blk, inv_width, inv_count):
    cand = cn_ref[blk]
    scores = lax.dot_general(
        xn, cand, (((1,), (1,)), ((), ())), preferred_element_type=jnp.float32
    )
    log2e = 1.0 / math.log(2.0)
    return jnp.exp2(scores * (inv_width * log2e) + (math.log2(inv_count) - OFFSET * log2e))


def sweep_body(nbr, inv_width, inv_count, bary, links_ref, xn_ref, cn_ref, scale_ref, mass_ref,
               *rest):
    if bary:
        rows_ref, ds_ref, ws_ref, kbuf = rest
    else:
        ds_ref, ct_ref, kbuf = rest
    b = pl.program_id(0)

    @pl.when(b == 0)
    def _():
        if bary:
            ws_ref[...] = jnp.zeros_like(ws_ref)
        else:
            ct_ref[...] = jnp.zeros_like(ct_ref)

    xn = xn_ref[...]
    acc = jnp.zeros((BLOCK, BLOCK), jnp.float32)
    for s in range(nbr):
        blk = links_ref[b, s]
        k = _kernel_slot(xn, cn_ref, blk, inv_width, inv_count)
        kbuf[s] = k
        acc = acc + k * scale_ref[pl.ds(blk, 1), :]
    row_total = jnp.sum(acc, axis=1, keepdims=True)
    ds = mass_ref[...] / row_total
    ds_ref[...] = ds
    if bary:
        rows = rows_ref[...]
    for s in range(nbr):
        blk = links_ref[b, s]
        k = kbuf[s]
        part = jnp.sum(k * ds, axis=0, keepdims=True)
        if bary:
            q = blk // 2
            half = pl.multiple_of((blk % 2) * BLOCK, BLOCK)
            ws_ref[q, pl.ds(2 * BLOCK, 1), pl.ds(half, BLOCK)] += part
            w = (k * ds).astype(jnp.bfloat16)
            ws_ref[q, pl.ds(half, BLOCK), :] += lax.dot_general(
                w, rows, (((0,), (0,)), ((), ())), preferred_element_type=jnp.float32
            )
        else:
            ct_ref[pl.ds(blk, 1), :] += part


def sweep(xn, cn_blocks, scale_blocks, mass_col, links, rows=None):
    local_rows, feature_count = xn.shape
    block_count = cn_blocks.shape[0]
    local_blocks, nbr = links.shape
    bary = rows is not None
    inv_width = 1.0 / (feature_count * EPS)
    inv_count = 1.0 / (nbr * BLOCK)
    in_specs = [
        pl.BlockSpec((BLOCK, feature_count), lambda b, L: (b, 0)),
        pl.BlockSpec((block_count, BLOCK, feature_count), lambda b, L: (0, 0, 0)),
        pl.BlockSpec((block_count, BLOCK), lambda b, L: (0, 0)),
        pl.BlockSpec((BLOCK, 1), lambda b, L: (b, 0)),
    ]
    out_specs = [pl.BlockSpec((BLOCK, 1), lambda b, L: (b, 0))]
    out_shape = [jax.ShapeDtypeStruct((local_rows, 1), jnp.float32)]
    packed_rows = 2 * BLOCK + PAD
    args = [links, xn, cn_blocks, scale_blocks, mass_col]
    if bary:
        in_specs.append(pl.BlockSpec((BLOCK, feature_count), lambda b, L: (b, 0)))
        packed = (block_count // 2, packed_rows, feature_count)
        out_specs.append(pl.BlockSpec(packed, lambda b, L: (0, 0, 0)))
        out_shape.append(jax.ShapeDtypeStruct(packed, jnp.float32))
        args.append(rows)
    else:
        out_specs.append(pl.BlockSpec((block_count, BLOCK), lambda b, L: (0, 0)))
        out_shape.append(jax.ShapeDtypeStruct((block_count, BLOCK), jnp.float32))
    flops = 2 * local_rows * nbr * BLOCK * feature_count * (2 if bary else 1)
    return pl.pallas_call(
        functools.partial(sweep_body, nbr, inv_width, inv_count, bary),
        grid_spec=pltpu.PrefetchScalarGridSpec(
            num_scalar_prefetch=1,
            grid=(local_blocks,),
            in_specs=in_specs,
            out_specs=out_specs,
            scratch_shapes=[pltpu.VMEM((nbr, BLOCK, BLOCK), jnp.float32)],
        ),
        out_shape=out_shape,
        compiler_params=pltpu.CompilerParams(
            dimension_semantics=("arbitrary",), vmem_limit_bytes=48 * 1024 * 1024
        ),
        cost_estimate=pl.CostEstimate(
            flops=flops,
            transcendentals=local_rows * nbr * BLOCK,
            bytes_accessed=block_count * BLOCK * feature_count * (2 + (4 if bary else 0))
            + local_rows * feature_count * (4 if bary else 2),
        ),
    )(*args)


def on_device(sizes, data_rows, data_mass, block_links, cand_rows, cand_mass):
    local_rows, feature_count = data_rows.shape
    local_cands = cand_rows.shape[0]
    row_devices = sizes["yh"] * sizes["x"] * sizes["c"]
    col_devices = sizes["z"] * sizes["yl"]
    cand_total = local_cands * col_devices
    block_count = cand_total // BLOCK
    mass_ratio = local_rows * row_devices / local_cands
    col_index = lax.axis_index("z") * sizes["yl"] + lax.axis_index("yl")
    own_start = col_index * local_cands
    gathered = lax.all_gather(
        lax.all_gather(normalize(cand_rows), "yl", axis=0, tiled=True), "z", axis=0, tiled=True
    )
    cn_blocks = gathered.reshape(block_count, BLOCK, feature_count)
    xn = normalize(data_rows)
    mass_col = data_mass.reshape(local_rows, 1)
    links = block_links.astype(jnp.int32)
    scale_blocks = jnp.ones((block_count, BLOCK), jnp.float32)
    for sweep_index in range(ITERS - 1):
        _, part_total = sweep(xn, cn_blocks, scale_blocks, mass_col, links)
        whole_total = butterfly_sum(part_total, TOTAL_ORDER, sizes)
        scale_blocks = mass_ratio * cand_mass.reshape(block_count, BLOCK) / whole_total
    ds_col, packed = sweep(xn, cn_blocks, scale_blocks, mass_col, links, rows=data_rows)
    joined = lax.psum_scatter(packed.reshape(-1, feature_count), COL_AXES, scatter_dimension=0, tiled=True)
    joined = butterfly_sum(joined, ("c", "x", "yh"), sizes)
    own_sums = joined[:local_cands]
    own_total = joined[local_cands]
    own_scale = mass_ratio * lax.dynamic_slice_in_dim(cand_mass, own_start, local_cands) / own_total
    new_support = own_sums / own_total[:, None]
    return (ds_col.reshape(local_rows), own_scale, new_support)


def solution(mesh):
    row_size, col_size = mesh.devices.shape
    fine = Mesh(mesh.devices.reshape(2, row_size // 4, 2, col_size // 2, 2), ALL_AXES)
    sizes = dict(fine.shape)
    placed = (
        P(ALL_AXES, None),
        P(ALL_AXES),
        P(ALL_AXES, None),
        P(COL_AXES, None),
        P(),
    )
    return jax.shard_map(
        functools.partial(on_device, sizes),
        mesh=fine,
        in_specs=placed,
        out_specs=(P(ALL_AXES), P(COL_AXES), P(COL_AXES, None)),
        check_vma=False,
    )
```

```python
import functools
import math

import jax
import jax.numpy as jnp
from jax import lax
from jax.experimental import pallas as pl
from jax.experimental.pallas import tpu as pltpu
from jax.sharding import Mesh
from jax.sharding import PartitionSpec as P

BLOCK = 128
ITERS = 3


EPS = 0.05
OFFSET = 1.0
PAD = 8
SUB = 4

ROW_AXES = ("yh", "x", "c")
COL_AXES = ("z", "yl")
ALL_AXES = ROW_AXES + COL_AXES
TOTAL_ORDER = ("c", "yl", "yh", "x", "z")


def normalize(matrix):
    values = matrix.astype(jnp.float32)
    return (values * lax.rsqrt(jnp.mean(values * values, axis=1, keepdims=True) + 1e-06)).astype(
        jnp.bfloat16
    )


def butterfly_sum(x, axes, sizes):
    for axis in axes:
        n = sizes[axis]
        k = 1
        while k < n:
            x = x + lax.ppermute(x, axis, [(j, j ^ k) for j in range(n)])
            k *= 2
    return x


def _kernel_slot(xn, cn_ref, blk, inv_width, inv_count):
    cand = cn_ref[blk]
    scores = lax.dot_general(
        xn, cand, (((1,), (1,)), ((), ())), preferred_element_type=jnp.float32
    )
    log2e = 1.0 / math.log(2.0)
    return jnp.exp2(scores * (inv_width * log2e) + (math.log2(inv_count) - OFFSET * log2e))


def sweep_body(nbr, inv_width, inv_count, bary, links_ref, xn_ref, cn_ref, scale_ref, mass_ref,
               *rest):
    if bary:
        rows_ref, ds_ref, ws_ref, kbuf = rest
    else:
        ds_ref, ct_ref, kbuf = rest
    b = pl.program_id(0)

    @pl.when(b == 0)
    def _():
        if bary:
            ws_ref[...] = jnp.zeros_like(ws_ref)
        else:
            ct_ref[...] = jnp.zeros_like(ct_ref)

    for u in range(SUB):
        step = b * SUB + u
        lo = u * BLOCK
        xn = xn_ref[pl.ds(lo, BLOCK), :]
        acc = jnp.zeros((BLOCK, BLOCK), jnp.float32)
        for s in range(nbr):
            blk = links_ref[step, s]
            k = _kernel_slot(xn, cn_ref, blk, inv_width, inv_count)
            kbuf[u, s] = k
            acc = acc + k * scale_ref[pl.ds(blk, 1), :]
        row_total = jnp.sum(acc, axis=1, keepdims=True)
        ds = mass_ref[pl.ds(lo, BLOCK), :] / row_total
        ds_ref[pl.ds(lo, BLOCK), :] = ds
        if bary:
            rows = rows_ref[pl.ds(lo, BLOCK), :]
        for s in range(nbr):
            blk = links_ref[step, s]
            k = kbuf[u, s]
            part = jnp.sum(k * ds, axis=0, keepdims=True)
            if bary:
                q = blk // 2
                half = pl.multiple_of((blk % 2) * BLOCK, BLOCK)
                ws_ref[q, pl.ds(2 * BLOCK, 1), pl.ds(half, BLOCK)] += part
                w = (k * ds).astype(jnp.bfloat16)
                ws_ref[q, pl.ds(half, BLOCK), :] += lax.dot_general(
                    w, rows, (((0,), (0,)), ((), ())), preferred_element_type=jnp.float32
                )
            else:
                ct_ref[pl.ds(blk, 1), :] += part


def sweep(xn, cn_blocks, scale_blocks, mass_col, links, rows=None):
    local_rows, feature_count = xn.shape
    block_count = cn_blocks.shape[0]
    local_blocks, nbr = links.shape
    bary = rows is not None
    inv_width = 1.0 / (feature_count * EPS)
    inv_count = 1.0 / (nbr * BLOCK)
    in_specs = [
        pl.BlockSpec((SUB * BLOCK, feature_count), lambda b, L: (b, 0)),
        pl.BlockSpec((block_count, BLOCK, feature_count), lambda b, L: (0, 0, 0)),
        pl.BlockSpec((block_count, BLOCK), lambda b, L: (0, 0)),
        pl.BlockSpec((SUB * BLOCK, 1), lambda b, L: (b, 0)),
    ]
    out_specs = [pl.BlockSpec((SUB * BLOCK, 1), lambda b, L: (b, 0))]
    out_shape = [jax.ShapeDtypeStruct((local_rows, 1), jnp.float32)]
    packed_rows = 2 * BLOCK + PAD
    args = [links, xn, cn_blocks, scale_blocks, mass_col]
    if bary:
        in_specs.append(pl.BlockSpec((SUB * BLOCK, feature_count), lambda b, L: (b, 0)))
        packed = (block_count // 2, packed_rows, feature_count)
        out_specs.append(pl.BlockSpec(packed, lambda b, L: (0, 0, 0)))
        out_shape.append(jax.ShapeDtypeStruct(packed, jnp.float32))
        args.append(rows)
    else:
        out_specs.append(pl.BlockSpec((block_count, BLOCK), lambda b, L: (0, 0)))
        out_shape.append(jax.ShapeDtypeStruct((block_count, BLOCK), jnp.float32))
    flops = 2 * local_rows * nbr * BLOCK * feature_count * (2 if bary else 1)
    return pl.pallas_call(
        functools.partial(sweep_body, nbr, inv_width, inv_count, bary),
        grid_spec=pltpu.PrefetchScalarGridSpec(
            num_scalar_prefetch=1,
            grid=(local_blocks // SUB,),
            in_specs=in_specs,
            out_specs=out_specs,
            scratch_shapes=[pltpu.VMEM((SUB, nbr, BLOCK, BLOCK), jnp.float32)],
        ),
        out_shape=out_shape,
        compiler_params=pltpu.CompilerParams(
            dimension_semantics=("arbitrary",), vmem_limit_bytes=48 * 1024 * 1024
        ),
        cost_estimate=pl.CostEstimate(
            flops=flops,
            transcendentals=local_rows * nbr * BLOCK,
            bytes_accessed=block_count * BLOCK * feature_count * (2 + (4 if bary else 0))
            + local_rows * feature_count * (4 if bary else 2),
        ),
    )(*args)


def on_device(sizes, data_rows, data_mass, block_links, cand_rows, cand_mass):
    local_rows, feature_count = data_rows.shape
    local_cands = cand_rows.shape[0]
    row_devices = sizes["yh"] * sizes["x"] * sizes["c"]
    col_devices = sizes["z"] * sizes["yl"]
    cand_total = local_cands * col_devices
    block_count = cand_total // BLOCK
    mass_ratio = local_rows * row_devices / local_cands
    col_index = lax.axis_index("z") * sizes["yl"] + lax.axis_index("yl")
    own_start = col_index * local_cands
    gathered = lax.all_gather(
        lax.all_gather(normalize(cand_rows), "yl", axis=0, tiled=True), "z", axis=0, tiled=True
    )
    cn_blocks = gathered.reshape(block_count, BLOCK, feature_count)
    xn = normalize(data_rows)
    mass_col = data_mass.reshape(local_rows, 1)
    links = block_links.astype(jnp.int32)
    scale_blocks = jnp.ones((block_count, BLOCK), jnp.float32)
    for sweep_index in range(ITERS - 1):
        _, part_total = sweep(xn, cn_blocks, scale_blocks, mass_col, links)
        whole_total = butterfly_sum(part_total, TOTAL_ORDER, sizes)
        scale_blocks = mass_ratio * cand_mass.reshape(block_count, BLOCK) / whole_total
    ds_col, packed = sweep(xn, cn_blocks, scale_blocks, mass_col, links, rows=data_rows)
    joined = lax.psum_scatter(packed.reshape(-1, feature_count), COL_AXES, scatter_dimension=0, tiled=True)
    joined = butterfly_sum(joined, ("c", "x", "yh"), sizes)
    own_sums = joined[:local_cands]
    own_total = joined[local_cands]
    own_scale = mass_ratio * lax.dynamic_slice_in_dim(cand_mass, own_start, local_cands) / own_total
    new_support = own_sums / own_total[:, None]
    return (ds_col.reshape(local_rows), own_scale, new_support)


def solution(mesh):
    row_size, col_size = mesh.devices.shape
    fine = Mesh(mesh.devices.reshape(2, row_size // 4, 2, col_size // 2, 2), ALL_AXES)
    sizes = dict(fine.shape)
    placed = (
        P(ALL_AXES, None),
        P(ALL_AXES),
        P(ALL_AXES, None),
        P(COL_AXES, None),
        P(),
    )
    return jax.shard_map(
        functools.partial(on_device, sizes),
        mesh=fine,
        in_specs=placed,
        out_specs=(P(ALL_AXES), P(COL_AXES), P(COL_AXES, None)),
        check_vma=False,
    )
```

```python
import functools
import math

import jax
import jax.numpy as jnp
from jax import lax
from jax.experimental import pallas as pl
from jax.experimental.pallas import tpu as pltpu
from jax.sharding import Mesh
from jax.sharding import PartitionSpec as P

BLOCK = 128
ITERS = 3


EPS = 0.05
OFFSET = 1.0
PAD = 8
SUB = 4

ROW_AXES = ("yh", "x", "c")
COL_AXES = ("z", "yl")
ALL_AXES = ROW_AXES + COL_AXES
TOTAL_ORDER = ("c", "yl", "yh", "x", "z")


def normalize(matrix):
    values = matrix.astype(jnp.float32)
    return (values * lax.rsqrt(jnp.mean(values * values, axis=1, keepdims=True) + 1e-06)).astype(
        jnp.bfloat16
    )


def butterfly_sum(x, axes, sizes):
    for axis in axes:
        n = sizes[axis]
        k = 1
        while k < n:
            x = x + lax.ppermute(x, axis, [(j, j ^ k) for j in range(n)])
            k *= 2
    return x


def _kernel_slot(xn, cn_ref, blk, inv_width, inv_count):
    cand = cn_ref[blk]
    scores = lax.dot_general(
        xn, cand, (((1,), (1,)), ((), ())), preferred_element_type=jnp.float32
    )
    log2e = 1.0 / math.log(2.0)
    return jnp.exp2(scores * (inv_width * log2e) + (math.log2(inv_count) - OFFSET * log2e))


def sweep_body(nbr, inv_width, inv_count, bary, links_ref, xn_ref, cn_ref, scale_ref, mass_ref,
               *rest):
    if bary:
        rows_ref, ds_ref, ws_ref, kbuf = rest
    else:
        ds_ref, ct_ref, kbuf = rest
    b = pl.program_id(0)

    @pl.when(b == 0)
    def _():
        if bary:
            ws_ref[...] = jnp.zeros_like(ws_ref)
        else:
            ct_ref[...] = jnp.zeros_like(ct_ref)

    for u in range(SUB):
        step = b * SUB + u
        lo = u * BLOCK
        xn = xn_ref[pl.ds(lo, BLOCK), :]
        acc = jnp.zeros((BLOCK, BLOCK), jnp.float32)
        for s in range(nbr):
            blk = links_ref[step, s]
            k = _kernel_slot(xn, cn_ref, blk, inv_width, inv_count)
            kbuf[u, s] = k
            acc = acc + k * scale_ref[pl.ds(blk, 1), :]
        row_total = jnp.sum(acc, axis=1, keepdims=True)
        ds = mass_ref[pl.ds(lo, BLOCK), :] / row_total
        ds_ref[pl.ds(lo, BLOCK), :] = ds
        if bary:
            rows = rows_ref[pl.ds(lo, BLOCK), :]
        for s in range(nbr):
            blk = links_ref[step, s]
            k = kbuf[u, s]
            part = jnp.sum(k * ds, axis=0, keepdims=True)
            if bary:
                q = blk // 2
                half = pl.multiple_of((blk % 2) * BLOCK, BLOCK)
                ws_ref[q, pl.ds(2 * BLOCK, 1), pl.ds(half, BLOCK)] += part
                w = (k * ds).astype(jnp.bfloat16)
                ws_ref[q, pl.ds(half, BLOCK), :] += lax.dot_general(
                    w, rows, (((0,), (0,)), ((), ())), preferred_element_type=jnp.float32
                )
            else:
                ct_ref[pl.ds(blk, 1), :] += part


def sweep(xn, cn_blocks, scale_blocks, mass_col, links, rows=None):
    local_rows, feature_count = xn.shape
    block_count = cn_blocks.shape[0]
    local_blocks, nbr = links.shape
    bary = rows is not None
    inv_width = 1.0 / (feature_count * EPS)
    inv_count = 1.0 / (nbr * BLOCK)
    in_specs = [
        pl.BlockSpec((SUB * BLOCK, feature_count), lambda b, L: (b, 0)),
        pl.BlockSpec((block_count, BLOCK, feature_count), lambda b, L: (0, 0, 0)),
        pl.BlockSpec((block_count, BLOCK), lambda b, L: (0, 0)),
        pl.BlockSpec((SUB * BLOCK, 1), lambda b, L: (b, 0)),
    ]
    out_specs = [pl.BlockSpec((SUB * BLOCK, 1), lambda b, L: (b, 0))]
    out_shape = [jax.ShapeDtypeStruct((local_rows, 1), jnp.float32)]
    packed_rows = 2 * BLOCK + PAD
    args = [links, xn, cn_blocks, scale_blocks, mass_col]
    if bary:
        in_specs.append(pl.BlockSpec((SUB * BLOCK, feature_count), lambda b, L: (b, 0)))
        packed = (block_count // 2, packed_rows, feature_count)
        out_specs.append(pl.BlockSpec(packed, lambda b, L: (0, 0, 0)))
        out_shape.append(jax.ShapeDtypeStruct(packed, jnp.float32))
        args.append(rows)
    else:
        out_specs.append(pl.BlockSpec((block_count, BLOCK), lambda b, L: (0, 0)))
        out_shape.append(jax.ShapeDtypeStruct((block_count, BLOCK), jnp.float32))
    flops = 2 * local_rows * nbr * BLOCK * feature_count * (2 if bary else 1)
    return pl.pallas_call(
        functools.partial(sweep_body, nbr, inv_width, inv_count, bary),
        grid_spec=pltpu.PrefetchScalarGridSpec(
            num_scalar_prefetch=1,
            grid=(local_blocks // SUB,),
            in_specs=in_specs,
            out_specs=out_specs,
            scratch_shapes=[pltpu.VMEM((SUB, nbr, BLOCK, BLOCK), jnp.float32)],
        ),
        out_shape=out_shape,
        compiler_params=pltpu.CompilerParams(
            dimension_semantics=("arbitrary",), vmem_limit_bytes=48 * 1024 * 1024
        ),
        cost_estimate=pl.CostEstimate(
            flops=flops,
            transcendentals=local_rows * nbr * BLOCK,
            bytes_accessed=block_count * BLOCK * feature_count * (2 + (4 if bary else 0))
            + local_rows * feature_count * (4 if bary else 2),
        ),
    )(*args)


def on_device(sizes, data_rows, data_mass, block_links, cand_rows, cand_mass):
    local_rows, feature_count = data_rows.shape
    local_cands = cand_rows.shape[0]
    row_devices = sizes["yh"] * sizes["x"] * sizes["c"]
    col_devices = sizes["z"] * sizes["yl"]
    cand_total = local_cands * col_devices
    block_count = cand_total // BLOCK
    mass_ratio = local_rows * row_devices / local_cands
    col_index = lax.axis_index("z") * sizes["yl"] + lax.axis_index("yl")
    own_start = col_index * local_cands
    own_cn = normalize(cand_rows)
    pair_cn = lax.ppermute(own_cn, "yl", [(0, 1), (1, 0)])
    first_lo = lax.axis_index("yl") == 0
    slab = jnp.concatenate(
        [jnp.where(first_lo, own_cn, pair_cn), jnp.where(first_lo, pair_cn, own_cn)], axis=0
    )
    gathered = lax.all_gather(slab, "z", axis=0, tiled=True)
    cn_blocks = gathered.reshape(block_count, BLOCK, feature_count)
    xn = normalize(data_rows)
    mass_col = data_mass.reshape(local_rows, 1)
    links = block_links.astype(jnp.int32)
    scale_blocks = jnp.ones((block_count, BLOCK), jnp.float32)
    for sweep_index in range(ITERS - 1):
        _, part_total = sweep(xn, cn_blocks, scale_blocks, mass_col, links)
        whole_total = butterfly_sum(part_total, TOTAL_ORDER, sizes)
        scale_blocks = mass_ratio * cand_mass.reshape(block_count, BLOCK) / whole_total
    ds_col, packed = sweep(xn, cn_blocks, scale_blocks, mass_col, links, rows=data_rows)
    joined = lax.psum_scatter(packed.reshape(-1, feature_count), COL_AXES, scatter_dimension=0, tiled=True)
    first_core = lax.axis_index("c") == 0
    sums_a, sums_b, totals = joined[:BLOCK], joined[BLOCK:2 * BLOCK], joined[2 * BLOCK:]
    keep = jnp.concatenate([jnp.where(first_core, sums_a, sums_b), totals], axis=0)
    give = jnp.concatenate([jnp.where(first_core, sums_b, sums_a), totals], axis=0)
    mine = keep + lax.ppermute(give, "c", [(0, 1), (1, 0)])
    mine = butterfly_sum(mine, ("x", "yh"), sizes)
    other = lax.ppermute(mine, "c", [(0, 1), (1, 0)])
    low = jnp.where(first_core, mine, other)
    high = jnp.where(first_core, other, mine)
    own_sums = jnp.concatenate([low[:BLOCK], high[:BLOCK]], axis=0)
    own_total = low[BLOCK]
    own_scale = mass_ratio * lax.dynamic_slice_in_dim(cand_mass, own_start, local_cands) / own_total
    new_support = own_sums / own_total[:, None]
    return (ds_col.reshape(local_rows), own_scale, new_support)


def solution(mesh):
    row_size, col_size = mesh.devices.shape
    fine = Mesh(mesh.devices.reshape(2, row_size // 4, 2, col_size // 2, 2), ALL_AXES)
    sizes = dict(fine.shape)
    placed = (
        P(ALL_AXES, None),
        P(ALL_AXES),
        P(ALL_AXES, None),
        P(COL_AXES, None),
        P(),
    )
    return jax.shard_map(
        functools.partial(on_device, sizes),
        mesh=fine,
        in_specs=placed,
        out_specs=(P(ALL_AXES), P(COL_AXES), P(COL_AXES, None)),
        check_vma=False,
    )
```

```python
import functools
import math

import jax
import jax.numpy as jnp
from jax import lax
from jax.experimental import pallas as pl
from jax.experimental.pallas import tpu as pltpu
from jax.sharding import Mesh
from jax.sharding import PartitionSpec as P

BLOCK = 128
ITERS = 3


EPS = 0.05
OFFSET = 1.0
PAD = 8
SUB = 4

ROW_AXES = ("yh", "x", "c")
COL_AXES = ("z", "yl")
ALL_AXES = ROW_AXES + COL_AXES
TOTAL_ORDER = ("c", "yl", "yh", "x", "z")


def normalize(matrix):
    values = matrix.astype(jnp.float32)
    return (values * lax.rsqrt(jnp.mean(values * values, axis=1, keepdims=True) + 1e-06)).astype(
        jnp.bfloat16
    )


def butterfly_sum(x, axes, sizes):
    for axis in axes:
        n = sizes[axis]
        k = 1
        while k < n:
            x = x + lax.ppermute(x, axis, [(j, j ^ k) for j in range(n)])
            k *= 2
    return x


def _kernel_slot(xn, cn_ref, blk, inv_width, inv_count):
    cand = cn_ref[blk]
    scores = lax.dot_general(
        xn, cand, (((1,), (1,)), ((), ())), preferred_element_type=jnp.float32
    )
    log2e = 1.0 / math.log(2.0)
    return jnp.exp2(scores * (inv_width * log2e) + (math.log2(inv_count) - OFFSET * log2e))


def sweep_body(nbr, inv_width, inv_count, bary, links_ref, xn_ref, cn_ref, scale_ref, mass_ref,
               *rest):
    if bary:
        rows_ref, ds_ref, ws_ref, kbuf = rest
    else:
        ds_ref, ct_ref, kbuf = rest
    b = pl.program_id(0)

    @pl.when(b == 0)
    def _():
        if bary:
            ws_ref[...] = jnp.zeros_like(ws_ref)
        else:
            ct_ref[...] = jnp.zeros_like(ct_ref)

    for u in range(SUB):
        step = b * SUB + u
        lo = u * BLOCK
        xn = xn_ref[pl.ds(lo, BLOCK), :]
        acc = jnp.zeros((BLOCK, BLOCK), jnp.float32)
        for s in range(nbr):
            blk = links_ref[step, s]
            k = _kernel_slot(xn, cn_ref, blk, inv_width, inv_count)
            kbuf[u, s] = k
            acc = acc + k * scale_ref[pl.ds(blk, 1), :]
        row_total = jnp.sum(acc, axis=1, keepdims=True)
        ds = mass_ref[pl.ds(lo, BLOCK), :] / row_total
        ds_ref[pl.ds(lo, BLOCK), :] = ds
        if bary:
            rows = rows_ref[pl.ds(lo, BLOCK), :]
        for s in range(nbr):
            blk = links_ref[step, s]
            k = kbuf[u, s]
            part = jnp.sum(k * ds, axis=0, keepdims=True)
            if bary:
                q = blk // 2
                half = pl.multiple_of((blk % 2) * BLOCK, BLOCK)
                ws_ref[q, pl.ds(2 * BLOCK, 1), pl.ds(half, BLOCK)] += part
                w = (k * ds).astype(jnp.bfloat16)
                ws_ref[q, pl.ds(half, BLOCK), :] += lax.dot_general(
                    w, rows, (((0,), (0,)), ((), ())), preferred_element_type=jnp.float32
                )
            else:
                ct_ref[pl.ds(blk, 1), :] += part


def sweep(xn, cn_blocks, scale_blocks, mass_col, links, rows=None):
    local_rows, feature_count = xn.shape
    block_count = cn_blocks.shape[0]
    local_blocks, nbr = links.shape
    bary = rows is not None
    inv_width = 1.0 / (feature_count * EPS)
    inv_count = 1.0 / (nbr * BLOCK)
    in_specs = [
        pl.BlockSpec((SUB * BLOCK, feature_count), lambda b, L: (b, 0)),
        pl.BlockSpec((block_count, BLOCK, feature_count), lambda b, L: (0, 0, 0)),
        pl.BlockSpec((block_count, BLOCK), lambda b, L: (0, 0)),
        pl.BlockSpec((SUB * BLOCK, 1), lambda b, L: (b, 0)),
    ]
    out_specs = [pl.BlockSpec((SUB * BLOCK, 1), lambda b, L: (b, 0))]
    out_shape = [jax.ShapeDtypeStruct((local_rows, 1), jnp.float32)]
    packed_rows = 2 * BLOCK + PAD
    args = [links, xn, cn_blocks, scale_blocks, mass_col]
    if bary:
        in_specs.append(pl.BlockSpec((SUB * BLOCK, feature_count), lambda b, L: (b, 0)))
        packed = (block_count // 2, packed_rows, feature_count)
        out_specs.append(pl.BlockSpec(packed, lambda b, L: (0, 0, 0)))
        out_shape.append(jax.ShapeDtypeStruct(packed, jnp.float32))
        args.append(rows)
    else:
        out_specs.append(pl.BlockSpec((block_count, BLOCK), lambda b, L: (0, 0)))
        out_shape.append(jax.ShapeDtypeStruct((block_count, BLOCK), jnp.float32))
    flops = 2 * local_rows * nbr * BLOCK * feature_count * (2 if bary else 1)
    return pl.pallas_call(
        functools.partial(sweep_body, nbr, inv_width, inv_count, bary),
        grid_spec=pltpu.PrefetchScalarGridSpec(
            num_scalar_prefetch=1,
            grid=(local_blocks // SUB,),
            in_specs=in_specs,
            out_specs=out_specs,
            scratch_shapes=[pltpu.VMEM((SUB, nbr, BLOCK, BLOCK), jnp.float32)],
        ),
        out_shape=out_shape,
        compiler_params=pltpu.CompilerParams(
            dimension_semantics=("arbitrary",), vmem_limit_bytes=48 * 1024 * 1024
        ),
        cost_estimate=pl.CostEstimate(
            flops=flops,
            transcendentals=local_rows * nbr * BLOCK,
            bytes_accessed=block_count * BLOCK * feature_count * (2 + (4 if bary else 0))
            + local_rows * feature_count * (4 if bary else 2),
        ),
    )(*args)


def on_device(sizes, data_rows, data_mass, block_links, cand_rows, cand_mass):
    local_rows, feature_count = data_rows.shape
    local_cands = cand_rows.shape[0]
    row_devices = sizes["yh"] * sizes["x"] * sizes["c"]
    col_devices = sizes["z"] * sizes["yl"]
    cand_total = local_cands * col_devices
    block_count = cand_total // BLOCK
    mass_ratio = local_rows * row_devices / local_cands
    col_index = lax.axis_index("z") * sizes["yl"] + lax.axis_index("yl")
    own_start = col_index * local_cands
    own_cn = normalize(cand_rows)
    pair_cn = lax.ppermute(own_cn, "yl", [(0, 1), (1, 0)])
    first_lo = lax.axis_index("yl") == 0
    slab = jnp.concatenate(
        [jnp.where(first_lo, own_cn, pair_cn), jnp.where(first_lo, pair_cn, own_cn)], axis=0
    )
    gathered = lax.all_gather(slab, "z", axis=0, tiled=True)
    cn_blocks = gathered.reshape(block_count, BLOCK, feature_count)
    xn = normalize(data_rows)
    mass_col = data_mass.reshape(local_rows, 1)
    links = block_links.astype(jnp.int32)
    scale_blocks = jnp.ones((block_count, BLOCK), jnp.float32)
    for sweep_index in range(ITERS - 1):
        _, part_total = sweep(xn, cn_blocks, scale_blocks, mass_col, links)
        whole_total = butterfly_sum(part_total, TOTAL_ORDER, sizes)
        scale_blocks = mass_ratio * cand_mass.reshape(block_count, BLOCK) / whole_total
    ds_col, packed = sweep(xn, cn_blocks, scale_blocks, mass_col, links, rows=data_rows)
    pair = lax.psum_scatter(packed.reshape(-1, feature_count), "z", scatter_dimension=0, tiled=True)
    part_rows = pair.shape[0] // 2
    first_lo = lax.axis_index("yl") == 0
    keep = jnp.where(first_lo, pair[:part_rows], pair[part_rows:])
    give = jnp.where(first_lo, pair[part_rows:], pair[:part_rows])
    joined = keep + lax.ppermute(give, "yl", [(0, 1), (1, 0)])
    first_core = lax.axis_index("c") == 0
    sums_a, sums_b, totals = joined[:BLOCK], joined[BLOCK:2 * BLOCK], joined[2 * BLOCK:]
    keep = jnp.concatenate([jnp.where(first_core, sums_a, sums_b), totals], axis=0)
    give = jnp.concatenate([jnp.where(first_core, sums_b, sums_a), totals], axis=0)
    mine = keep + lax.ppermute(give, "c", [(0, 1), (1, 0)])
    mine = butterfly_sum(mine, ("x", "yh"), sizes)
    other = lax.ppermute(mine, "c", [(0, 1), (1, 0)])
    low = jnp.where(first_core, mine, other)
    high = jnp.where(first_core, other, mine)
    own_sums = jnp.concatenate([low[:BLOCK], high[:BLOCK]], axis=0)
    own_total = low[BLOCK]
    own_scale = mass_ratio * lax.dynamic_slice_in_dim(cand_mass, own_start, local_cands) / own_total
    new_support = own_sums / own_total[:, None]
    return (ds_col.reshape(local_rows), own_scale, new_support)


def solution(mesh):
    row_size, col_size = mesh.devices.shape
    fine = Mesh(mesh.devices.reshape(2, row_size // 4, 2, col_size // 2, 2), ALL_AXES)
    sizes = dict(fine.shape)
    placed = (
        P(ALL_AXES, None),
        P(ALL_AXES),
        P(ALL_AXES, None),
        P(COL_AXES, None),
        P(),
    )
    return jax.shard_map(
        functools.partial(on_device, sizes),
        mesh=fine,
        in_specs=placed,
        out_specs=(P(ALL_AXES), P(COL_AXES), P(COL_AXES, None)),
        check_vma=False,
    )
```

```python
import functools
import math

import jax
import jax.numpy as jnp
from jax import lax
from jax.experimental import pallas as pl
from jax.experimental.pallas import tpu as pltpu
from jax.sharding import Mesh
from jax.sharding import PartitionSpec as P

BLOCK = 128
ITERS = 3


EPS = 0.05
OFFSET = 1.0
PAD = 8
SUB = 4
Z_LO = 4

ROW_AXES = ("yh", "x", "c")
COL_AXES = ("zh", "zl", "yl")
ALL_AXES = ROW_AXES + COL_AXES
TOTAL_ORDER = ("c", "yl", "yh", "x", "zl", "zh")


def normalize(matrix):
    values = matrix.astype(jnp.float32)
    return (values * lax.rsqrt(jnp.mean(values * values, axis=1, keepdims=True) + 1e-06)).astype(
        jnp.bfloat16
    )


def butterfly_sum(x, axes, sizes):
    for axis in axes:
        n = sizes[axis]
        k = 1
        while k < n:
            x = x + lax.ppermute(x, axis, [(j, j ^ k) for j in range(n)])
            k *= 2
    return x


def _kernel_slot(xn, cn_ref, blk, inv_width, inv_count):
    cand = cn_ref[blk]
    scores = lax.dot_general(
        xn, cand, (((1,), (1,)), ((), ())), preferred_element_type=jnp.float32
    )
    log2e = 1.0 / math.log(2.0)
    return jnp.exp2(scores * (inv_width * log2e) + (math.log2(inv_count) - OFFSET * log2e))


def sweep_body(nbr, inv_width, inv_count, bary, links_ref, xn_ref, cn_ref, scale_ref, mass_ref,
               *rest):
    if bary:
        rows_ref, ds_ref, ws_ref, kbuf = rest
    else:
        ds_ref, ct_ref, kbuf = rest
    b = pl.program_id(0)

    @pl.when(b == 0)
    def _():
        if bary:
            ws_ref[...] = jnp.zeros_like(ws_ref)
        else:
            ct_ref[...] = jnp.zeros_like(ct_ref)

    for u in range(SUB):
        step = b * SUB + u
        lo = u * BLOCK
        xn = xn_ref[pl.ds(lo, BLOCK), :]
        acc = jnp.zeros((BLOCK, BLOCK), jnp.float32)
        for s in range(nbr):
            blk = links_ref[step, s]
            k = _kernel_slot(xn, cn_ref, blk, inv_width, inv_count)
            kbuf[u, s] = k
            acc = acc + k * scale_ref[pl.ds(blk, 1), :]
        row_total = jnp.sum(acc, axis=1, keepdims=True)
        ds = mass_ref[pl.ds(lo, BLOCK), :] / row_total
        ds_ref[pl.ds(lo, BLOCK), :] = ds
        if bary:
            rows = rows_ref[pl.ds(lo, BLOCK), :]
        for s in range(nbr):
            blk = links_ref[step, s]
            k = kbuf[u, s]
            part = jnp.sum(k * ds, axis=0, keepdims=True)
            if bary:
                q = blk // 2
                zq = q // 2
                q = ((zq % Z_LO) * (ws_ref.shape[0] // (2 * Z_LO)) + zq // Z_LO) * 2 + q % 2
                half = pl.multiple_of((blk % 2) * BLOCK, BLOCK)
                ws_ref[q, pl.ds(2 * BLOCK, 1), pl.ds(half, BLOCK)] += part
                w = (k * ds).astype(jnp.bfloat16)
                ws_ref[q, pl.ds(half, BLOCK), :] += lax.dot_general(
                    w, rows, (((0,), (0,)), ((), ())), preferred_element_type=jnp.float32
                )
            else:
                ct_ref[pl.ds(blk, 1), :] += part


def sweep(xn, cn_blocks, scale_blocks, mass_col, links, rows=None):
    local_rows, feature_count = xn.shape
    block_count = cn_blocks.shape[0]
    local_blocks, nbr = links.shape
    bary = rows is not None
    inv_width = 1.0 / (feature_count * EPS)
    inv_count = 1.0 / (nbr * BLOCK)
    in_specs = [
        pl.BlockSpec((SUB * BLOCK, feature_count), lambda b, L: (b, 0)),
        pl.BlockSpec((block_count, BLOCK, feature_count), lambda b, L: (0, 0, 0)),
        pl.BlockSpec((block_count, BLOCK), lambda b, L: (0, 0)),
        pl.BlockSpec((SUB * BLOCK, 1), lambda b, L: (b, 0)),
    ]
    out_specs = [pl.BlockSpec((SUB * BLOCK, 1), lambda b, L: (b, 0))]
    out_shape = [jax.ShapeDtypeStruct((local_rows, 1), jnp.float32)]
    packed_rows = 2 * BLOCK + PAD
    args = [links, xn, cn_blocks, scale_blocks, mass_col]
    if bary:
        in_specs.append(pl.BlockSpec((SUB * BLOCK, feature_count), lambda b, L: (b, 0)))
        packed = (block_count // 2, packed_rows, feature_count)
        out_specs.append(pl.BlockSpec(packed, lambda b, L: (0, 0, 0)))
        out_shape.append(jax.ShapeDtypeStruct(packed, jnp.float32))
        args.append(rows)
    else:
        out_specs.append(pl.BlockSpec((block_count, BLOCK), lambda b, L: (0, 0)))
        out_shape.append(jax.ShapeDtypeStruct((block_count, BLOCK), jnp.float32))
    flops = 2 * local_rows * nbr * BLOCK * feature_count * (2 if bary else 1)
    return pl.pallas_call(
        functools.partial(sweep_body, nbr, inv_width, inv_count, bary),
        grid_spec=pltpu.PrefetchScalarGridSpec(
            num_scalar_prefetch=1,
            grid=(local_blocks // SUB,),
            in_specs=in_specs,
            out_specs=out_specs,
            scratch_shapes=[pltpu.VMEM((SUB, nbr, BLOCK, BLOCK), jnp.float32)],
        ),
        out_shape=out_shape,
        compiler_params=pltpu.CompilerParams(
            dimension_semantics=("arbitrary",), vmem_limit_bytes=48 * 1024 * 1024
        ),
        cost_estimate=pl.CostEstimate(
            flops=flops,
            transcendentals=local_rows * nbr * BLOCK,
            bytes_accessed=block_count * BLOCK * feature_count * (2 + (4 if bary else 0))
            + local_rows * feature_count * (4 if bary else 2),
        ),
    )(*args)


def on_device(sizes, data_rows, data_mass, block_links, cand_rows, cand_mass):
    local_rows, feature_count = data_rows.shape
    local_cands = cand_rows.shape[0]
    row_devices = sizes["yh"] * sizes["x"] * sizes["c"]
    col_devices = sizes["zh"] * sizes["zl"] * sizes["yl"]
    cand_total = local_cands * col_devices
    block_count = cand_total // BLOCK
    mass_ratio = local_rows * row_devices / local_cands
    col_index = (
        lax.axis_index("zh") * sizes["zl"] + lax.axis_index("zl")
    ) * sizes["yl"] + lax.axis_index("yl")
    own_start = col_index * local_cands
    own_cn = normalize(cand_rows)
    pair_cn = lax.ppermute(own_cn, "yl", [(0, 1), (1, 0)])
    first_lo = lax.axis_index("yl") == 0
    slab = jnp.concatenate(
        [jnp.where(first_lo, own_cn, pair_cn), jnp.where(first_lo, pair_cn, own_cn)], axis=0
    )
    gathered = lax.all_gather(slab, ("zh", "zl"), axis=0, tiled=True)
    cn_blocks = gathered.reshape(block_count, BLOCK, feature_count)
    xn = normalize(data_rows)
    mass_col = data_mass.reshape(local_rows, 1)
    links = block_links.astype(jnp.int32)
    scale_blocks = jnp.ones((block_count, BLOCK), jnp.float32)
    for sweep_index in range(ITERS - 1):
        _, part_total = sweep(xn, cn_blocks, scale_blocks, mass_col, links)
        whole_total = butterfly_sum(part_total, TOTAL_ORDER, sizes)
        scale_blocks = mass_ratio * cand_mass.reshape(block_count, BLOCK) / whole_total
    ds_col, packed = sweep(xn, cn_blocks, scale_blocks, mass_col, links, rows=data_rows)
    quad = lax.psum_scatter(packed.reshape(-1, feature_count), "zl", scatter_dimension=0, tiled=True)
    part_rows = quad.shape[0] // 4
    first_hi = lax.axis_index("zh") == 0
    keep = jnp.where(first_hi, quad[: 2 * part_rows], quad[2 * part_rows :])
    give = jnp.where(first_hi, quad[2 * part_rows :], quad[: 2 * part_rows])
    pair = keep + lax.ppermute(give, "zh", [(0, 1), (1, 0)])
    first_lo = lax.axis_index("yl") == 0
    keep = jnp.where(first_lo, pair[:part_rows], pair[part_rows:])
    give = jnp.where(first_lo, pair[part_rows:], pair[:part_rows])
    joined = keep + lax.ppermute(give, "yl", [(0, 1), (1, 0)])
    first_core = lax.axis_index("c") == 0
    sums_a, sums_b, totals = joined[:BLOCK], joined[BLOCK:2 * BLOCK], joined[2 * BLOCK:]
    keep = jnp.concatenate([jnp.where(first_core, sums_a, sums_b), totals], axis=0)
    give = jnp.concatenate([jnp.where(first_core, sums_b, sums_a), totals], axis=0)
    mine = keep + lax.ppermute(give, "c", [(0, 1), (1, 0)])
    mine = butterfly_sum(mine, ("x", "yh"), sizes)
    other = lax.ppermute(mine, "c", [(0, 1), (1, 0)])
    low = jnp.where(first_core, mine, other)
    high = jnp.where(first_core, other, mine)
    own_sums = jnp.concatenate([low[:BLOCK], high[:BLOCK]], axis=0)
    own_total = low[BLOCK]
    own_scale = mass_ratio * lax.dynamic_slice_in_dim(cand_mass, own_start, local_cands) / own_total
    new_support = own_sums / own_total[:, None]
    return (ds_col.reshape(local_rows), own_scale, new_support)


def solution(mesh):
    row_size, col_size = mesh.devices.shape
    fine = Mesh(
        mesh.devices.reshape(2, row_size // 4, 2, col_size // (2 * Z_LO), Z_LO, 2), ALL_AXES
    )
    sizes = dict(fine.shape)
    placed = (
        P(ALL_AXES, None),
        P(ALL_AXES),
        P(ALL_AXES, None),
        P(COL_AXES, None),
        P(),
    )
    return jax.shard_map(
        functools.partial(on_device, sizes),
        mesh=fine,
        in_specs=placed,
        out_specs=(P(ALL_AXES), P(COL_AXES), P(COL_AXES, None)),
        check_vma=False,
    )
```

```python
import functools
import math

import jax
import jax.numpy as jnp
from jax import lax
from jax.experimental import pallas as pl
from jax.experimental.pallas import tpu as pltpu
from jax.sharding import Mesh
from jax.sharding import PartitionSpec as P

BLOCK = 128
ITERS = 3


EPS = 0.05
OFFSET = 1.0
PAD = 8
SUB = 4

ROW_AXES = ("yh", "x", "c")
COL_AXES = ("z", "yl")
ALL_AXES = ROW_AXES + COL_AXES
TOTAL_ORDER = ("c", "yl", "yh", "x", "z")


def normalize(matrix):
    values = matrix.astype(jnp.float32)
    return (values * lax.rsqrt(jnp.mean(values * values, axis=1, keepdims=True) + 1e-06)).astype(
        jnp.bfloat16
    )


def butterfly_sum(x, axes, sizes):
    for axis in axes:
        n = sizes[axis]
        k = 1
        while k < n:
            x = x + lax.ppermute(x, axis, [(j, j ^ k) for j in range(n)])
            k *= 2
    return x


def _kernel_slot(xn, cn_ref, blk, inv_width, inv_count):
    cand = cn_ref[blk]
    scores = lax.dot_general(
        xn, cand, (((1,), (1,)), ((), ())), preferred_element_type=jnp.float32
    )
    log2e = 1.0 / math.log(2.0)
    return jnp.exp2(scores * (inv_width * log2e) + (math.log2(inv_count) - OFFSET * log2e))


def sweep_body(nbr, inv_width, inv_count, bary, links_ref, xn_ref, cn_ref, scale_ref, mass_ref,
               *rest):
    if bary:
        rows_ref, ds_ref, ws_ref, kbuf = rest
    else:
        ds_ref, ct_ref, kbuf = rest
    b = pl.program_id(0)

    @pl.when(b == 0)
    def _():
        if bary:
            ws_ref[...] = jnp.zeros_like(ws_ref)
        else:
            ct_ref[...] = jnp.zeros_like(ct_ref)

    for u in range(SUB):
        step = b * SUB + u
        lo = u * BLOCK
        xn = xn_ref[pl.ds(lo, BLOCK), :]
        acc = jnp.zeros((BLOCK, BLOCK), jnp.float32)
        for s in range(nbr):
            blk = links_ref[step, s]
            k = _kernel_slot(xn, cn_ref, blk, inv_width, inv_count)
            kbuf[u, s] = k
            acc = acc + k * scale_ref[pl.ds(blk, 1), :]
        row_total = jnp.sum(acc, axis=1, keepdims=True)
        ds = mass_ref[pl.ds(lo, BLOCK), :] / row_total
        ds_ref[pl.ds(lo, BLOCK), :] = ds
        if bary:
            rows = rows_ref[pl.ds(lo, BLOCK), :]
        for s in range(nbr):
            blk = links_ref[step, s]
            k = kbuf[u, s]
            part = jnp.sum(k * ds, axis=0, keepdims=True)
            if bary:
                q = blk // 2
                half = pl.multiple_of((blk % 2) * BLOCK, BLOCK)
                ws_ref[q, pl.ds(2 * BLOCK, 1), pl.ds(half, BLOCK)] += part
                w = (k * ds).astype(jnp.bfloat16)
                ws_ref[q, pl.ds(half, BLOCK), :] += lax.dot_general(
                    w, rows, (((0,), (0,)), ((), ())), preferred_element_type=jnp.float32
                )
            else:
                ct_ref[pl.ds(blk, 1), :] += part


def sweep(xn, cn_blocks, scale_blocks, mass_col, links, rows=None):
    local_rows, feature_count = xn.shape
    block_count = cn_blocks.shape[0]
    local_blocks, nbr = links.shape
    bary = rows is not None
    inv_width = 1.0 / (feature_count * EPS)
    inv_count = 1.0 / (nbr * BLOCK)
    in_specs = [
        pl.BlockSpec((SUB * BLOCK, feature_count), lambda b, L: (b, 0)),
        pl.BlockSpec((block_count, BLOCK, feature_count), lambda b, L: (0, 0, 0)),
        pl.BlockSpec((block_count, BLOCK), lambda b, L: (0, 0)),
        pl.BlockSpec((SUB * BLOCK, 1), lambda b, L: (b, 0)),
    ]
    out_specs = [pl.BlockSpec((SUB * BLOCK, 1), lambda b, L: (b, 0))]
    out_shape = [jax.ShapeDtypeStruct((local_rows, 1), jnp.float32)]
    packed_rows = 2 * BLOCK + PAD
    args = [links, xn, cn_blocks, scale_blocks, mass_col]
    if bary:
        in_specs.append(pl.BlockSpec((SUB * BLOCK, feature_count), lambda b, L: (b, 0)))
        packed = (block_count // 2, packed_rows, feature_count)
        out_specs.append(pl.BlockSpec(packed, lambda b, L: (0, 0, 0)))
        out_shape.append(jax.ShapeDtypeStruct(packed, jnp.float32))
        args.append(rows)
    else:
        out_specs.append(pl.BlockSpec((block_count, BLOCK), lambda b, L: (0, 0)))
        out_shape.append(jax.ShapeDtypeStruct((block_count, BLOCK), jnp.float32))
    flops = 2 * local_rows * nbr * BLOCK * feature_count * (2 if bary else 1)
    return pl.pallas_call(
        functools.partial(sweep_body, nbr, inv_width, inv_count, bary),
        grid_spec=pltpu.PrefetchScalarGridSpec(
            num_scalar_prefetch=1,
            grid=(local_blocks // SUB,),
            in_specs=in_specs,
            out_specs=out_specs,
            scratch_shapes=[pltpu.VMEM((SUB, nbr, BLOCK, BLOCK), jnp.float32)],
        ),
        out_shape=out_shape,
        compiler_params=pltpu.CompilerParams(
            dimension_semantics=("arbitrary",), vmem_limit_bytes=48 * 1024 * 1024
        ),
        cost_estimate=pl.CostEstimate(
            flops=flops,
            transcendentals=local_rows * nbr * BLOCK,
            bytes_accessed=block_count * BLOCK * feature_count * (2 + (4 if bary else 0))
            + local_rows * feature_count * (4 if bary else 2),
        ),
    )(*args)


def on_device(sizes, data_rows, data_mass, block_links, cand_rows, cand_mass):
    local_rows, feature_count = data_rows.shape
    local_cands = cand_rows.shape[0]
    row_devices = sizes["yh"] * sizes["x"] * sizes["c"]
    col_devices = sizes["z"] * sizes["yl"]
    cand_total = local_cands * col_devices
    block_count = cand_total // BLOCK
    mass_ratio = local_rows * row_devices / local_cands
    col_index = lax.axis_index("z") * sizes["yl"] + lax.axis_index("yl")
    own_start = col_index * local_cands
    own_cn = normalize(cand_rows)
    pair_cn = lax.ppermute(own_cn, "yl", [(0, 1), (1, 0)])
    first_lo = lax.axis_index("yl") == 0
    slab = jnp.concatenate(
        [jnp.where(first_lo, own_cn, pair_cn), jnp.where(first_lo, pair_cn, own_cn)], axis=0
    )
    gathered = lax.all_gather(slab, "z", axis=0, tiled=True)
    cn_blocks = gathered.reshape(block_count, BLOCK, feature_count)
    xn = normalize(data_rows)
    mass_col = data_mass.reshape(local_rows, 1)
    links = block_links.astype(jnp.int32)
    scale_blocks = jnp.ones((block_count, BLOCK), jnp.float32)
    for sweep_index in range(ITERS - 1):
        _, part_total = sweep(xn, cn_blocks, scale_blocks, mass_col, links)
        whole_total = butterfly_sum(part_total, TOTAL_ORDER, sizes)
        scale_blocks = mass_ratio * cand_mass.reshape(block_count, BLOCK) / whole_total
    ds_col, packed = sweep(xn, cn_blocks, scale_blocks, mass_col, links, rows=data_rows)
    pair = lax.psum_scatter(packed.reshape(-1, feature_count), "z", scatter_dimension=0, tiled=True)
    part_rows = pair.shape[0] // 2
    first_core = lax.axis_index("c") == 0
    keeps, gives = [], []
    for p in range(2):
        part = pair[p * part_rows:(p + 1) * part_rows]
        sums_a, sums_b, totals = part[:BLOCK], part[BLOCK:2 * BLOCK], part[2 * BLOCK:]
        keeps += [jnp.where(first_core, sums_a, sums_b), totals]
        gives += [jnp.where(first_core, sums_b, sums_a), totals]
    mine = jnp.concatenate(keeps, axis=0) + lax.ppermute(
        jnp.concatenate(gives, axis=0), "c", [(0, 1), (1, 0)]
    )
    quarter = mine.shape[0] // 2
    first_lo = lax.axis_index("yl") == 0
    keep = jnp.where(first_lo, mine[:quarter], mine[quarter:])
    give = jnp.where(first_lo, mine[quarter:], mine[:quarter])
    mine = keep + lax.ppermute(give, "yl", [(0, 1), (1, 0)])
    mine = butterfly_sum(mine, ("x", "yh"), sizes)
    other = lax.ppermute(mine, "c", [(0, 1), (1, 0)])
    low = jnp.where(first_core, mine, other)
    high = jnp.where(first_core, other, mine)
    own_sums = jnp.concatenate([low[:BLOCK], high[:BLOCK]], axis=0)
    own_total = low[BLOCK]
    own_scale = mass_ratio * lax.dynamic_slice_in_dim(cand_mass, own_start, local_cands) / own_total
    new_support = own_sums / own_total[:, None]
    return (ds_col.reshape(local_rows), own_scale, new_support)


def solution(mesh):
    row_size, col_size = mesh.devices.shape
    fine = Mesh(mesh.devices.reshape(2, row_size // 4, 2, col_size // 2, 2), ALL_AXES)
    sizes = dict(fine.shape)
    placed = (
        P(ALL_AXES, None),
        P(ALL_AXES),
        P(ALL_AXES, None),
        P(COL_AXES, None),
        P(),
    )
    return jax.shard_map(
        functools.partial(on_device, sizes),
        mesh=fine,
        in_specs=placed,
        out_specs=(P(ALL_AXES), P(COL_AXES), P(COL_AXES, None)),
        check_vma=False,
    )
```

```python
import functools
import math

import jax
import jax.numpy as jnp
from jax import lax
from jax.experimental import pallas as pl
from jax.experimental.pallas import tpu as pltpu
from jax.sharding import Mesh
from jax.sharding import PartitionSpec as P

BLOCK = 128
ITERS = 3


EPS = 0.05
OFFSET = 1.0
PAD = 8
SUB = 6

ROW_AXES = ("yh", "x", "c")
COL_AXES = ("z", "yl")
ALL_AXES = ROW_AXES + COL_AXES
TOTAL_ORDER = ("c", "yl", "yh", "x", "z")


def normalize(matrix):
    values = matrix.astype(jnp.float32)
    return (values * lax.rsqrt(jnp.mean(values * values, axis=1, keepdims=True) + 1e-06)).astype(
        jnp.bfloat16
    )


def butterfly_sum(x, axes, sizes):
    for axis in axes:
        n = sizes[axis]
        k = 1
        while k < n:
            x = x + lax.ppermute(x, axis, [(j, j ^ k) for j in range(n)])
            k *= 2
    return x


def _kernel_slot(xn, cn_ref, blk, inv_width, inv_count):
    cand = cn_ref[blk]
    scores = lax.dot_general(
        xn, cand, (((1,), (1,)), ((), ())), preferred_element_type=jnp.float32
    )
    log2e = 1.0 / math.log(2.0)
    return jnp.exp2(scores * (inv_width * log2e) + (math.log2(inv_count) - OFFSET * log2e))


def sweep_body(nbr, inv_width, inv_count, bary, links_ref, xn_ref, cn_ref, scale_ref, mass_ref,
               *rest):
    if bary:
        rows_ref, ds_ref, ws_ref, kbuf = rest
    else:
        ds_ref, ct_ref, kbuf = rest
    b = pl.program_id(0)

    @pl.when(b == 0)
    def _():
        if bary:
            ws_ref[...] = jnp.zeros_like(ws_ref)
        else:
            ct_ref[...] = jnp.zeros_like(ct_ref)

    for u in range(SUB):
        step = b * SUB + u
        lo = u * BLOCK
        xn = xn_ref[pl.ds(lo, BLOCK), :]
        acc = jnp.zeros((BLOCK, BLOCK), jnp.float32)
        for s in range(nbr):
            blk = links_ref[step, s]
            k = _kernel_slot(xn, cn_ref, blk, inv_width, inv_count)
            kbuf[u, s] = k
            acc = acc + k * scale_ref[pl.ds(blk, 1), :]
        row_total = jnp.sum(acc, axis=1, keepdims=True)
        ds = mass_ref[pl.ds(lo, BLOCK), :] / row_total
        ds_ref[pl.ds(lo, BLOCK), :] = ds
        if bary:
            rows = rows_ref[pl.ds(lo, BLOCK), :]
        for s in range(nbr):
            blk = links_ref[step, s]
            k = kbuf[u, s]
            part = jnp.sum(k * ds, axis=0, keepdims=True)
            if bary:
                q = blk // 2
                half = pl.multiple_of((blk % 2) * BLOCK, BLOCK)
                ws_ref[q, pl.ds(2 * BLOCK, 1), pl.ds(half, BLOCK)] += part
                w = (k * ds).astype(jnp.bfloat16)
                ws_ref[q, pl.ds(half, BLOCK), :] += lax.dot_general(
                    w, rows, (((0,), (0,)), ((), ())), preferred_element_type=jnp.float32
                )
            else:
                ct_ref[pl.ds(blk, 1), :] += part


def sweep(xn, cn_blocks, scale_blocks, mass_col, links, rows=None):
    local_rows, feature_count = xn.shape
    block_count = cn_blocks.shape[0]
    local_blocks, nbr = links.shape
    bary = rows is not None
    inv_width = 1.0 / (feature_count * EPS)
    inv_count = 1.0 / (nbr * BLOCK)
    in_specs = [
        pl.BlockSpec((SUB * BLOCK, feature_count), lambda b, L: (b, 0)),
        pl.BlockSpec((block_count, BLOCK, feature_count), lambda b, L: (0, 0, 0)),
        pl.BlockSpec((block_count, BLOCK), lambda b, L: (0, 0)),
        pl.BlockSpec((SUB * BLOCK, 1), lambda b, L: (b, 0)),
    ]
    out_specs = [pl.BlockSpec((SUB * BLOCK, 1), lambda b, L: (b, 0))]
    out_shape = [jax.ShapeDtypeStruct((local_rows, 1), jnp.float32)]
    packed_rows = 2 * BLOCK + PAD
    args = [links, xn, cn_blocks, scale_blocks, mass_col]
    if bary:
        in_specs.append(pl.BlockSpec((SUB * BLOCK, feature_count), lambda b, L: (b, 0)))
        packed = (block_count // 2, packed_rows, feature_count)
        out_specs.append(pl.BlockSpec(packed, lambda b, L: (0, 0, 0)))
        out_shape.append(jax.ShapeDtypeStruct(packed, jnp.float32))
        args.append(rows)
    else:
        out_specs.append(pl.BlockSpec((block_count, BLOCK), lambda b, L: (0, 0)))
        out_shape.append(jax.ShapeDtypeStruct((block_count, BLOCK), jnp.float32))
    flops = 2 * local_rows * nbr * BLOCK * feature_count * (2 if bary else 1)
    return pl.pallas_call(
        functools.partial(sweep_body, nbr, inv_width, inv_count, bary),
        grid_spec=pltpu.PrefetchScalarGridSpec(
            num_scalar_prefetch=1,
            grid=(local_blocks // SUB,),
            in_specs=in_specs,
            out_specs=out_specs,
            scratch_shapes=[pltpu.VMEM((SUB, nbr, BLOCK, BLOCK), jnp.float32)],
        ),
        out_shape=out_shape,
        compiler_params=pltpu.CompilerParams(
            dimension_semantics=("arbitrary",), vmem_limit_bytes=48 * 1024 * 1024
        ),
        cost_estimate=pl.CostEstimate(
            flops=flops,
            transcendentals=local_rows * nbr * BLOCK,
            bytes_accessed=block_count * BLOCK * feature_count * (2 + (4 if bary else 0))
            + local_rows * feature_count * (4 if bary else 2),
        ),
    )(*args)


def on_device(sizes, data_rows, data_mass, block_links, cand_rows, cand_mass):
    local_rows, feature_count = data_rows.shape
    local_cands = cand_rows.shape[0]
    row_devices = sizes["yh"] * sizes["x"] * sizes["c"]
    col_devices = sizes["z"] * sizes["yl"]
    cand_total = local_cands * col_devices
    block_count = cand_total // BLOCK
    mass_ratio = local_rows * row_devices / local_cands
    col_index = lax.axis_index("z") * sizes["yl"] + lax.axis_index("yl")
    own_start = col_index * local_cands
    own_cn = normalize(cand_rows)
    pair_cn = lax.ppermute(own_cn, "yl", [(0, 1), (1, 0)])
    first_lo = lax.axis_index("yl") == 0
    slab = jnp.concatenate(
        [jnp.where(first_lo, own_cn, pair_cn), jnp.where(first_lo, pair_cn, own_cn)], axis=0
    )
    gathered = lax.all_gather(slab, "z", axis=0, tiled=True)
    cn_blocks = gathered.reshape(block_count, BLOCK, feature_count)
    xn = normalize(data_rows)
    mass_col = data_mass.reshape(local_rows, 1)
    links = block_links.astype(jnp.int32)
    scale_blocks = jnp.ones((block_count, BLOCK), jnp.float32)
    for sweep_index in range(ITERS - 1):
        _, part_total = sweep(xn, cn_blocks, scale_blocks, mass_col, links)
        whole_total = butterfly_sum(part_total, TOTAL_ORDER, sizes)
        scale_blocks = mass_ratio * cand_mass.reshape(block_count, BLOCK) / whole_total
    ds_col, packed = sweep(xn, cn_blocks, scale_blocks, mass_col, links, rows=data_rows)
    pair = lax.psum_scatter(packed.reshape(-1, feature_count), "z", scatter_dimension=0, tiled=True)
    part_rows = pair.shape[0] // 2
    first_core = lax.axis_index("c") == 0
    keeps, gives = [], []
    for p in range(2):
        part = pair[p * part_rows:(p + 1) * part_rows]
        sums_a, sums_b, totals = part[:BLOCK], part[BLOCK:2 * BLOCK], part[2 * BLOCK:]
        keeps += [jnp.where(first_core, sums_a, sums_b), totals]
        gives += [jnp.where(first_core, sums_b, sums_a), totals]
    mine = jnp.concatenate(keeps, axis=0) + lax.ppermute(
        jnp.concatenate(gives, axis=0), "c", [(0, 1), (1, 0)]
    )
    quarter = mine.shape[0] // 2
    first_lo = lax.axis_index("yl") == 0
    keep = jnp.where(first_lo, mine[:quarter], mine[quarter:])
    give = jnp.where(first_lo, mine[quarter:], mine[:quarter])
    mine = keep + lax.ppermute(give, "yl", [(0, 1), (1, 0)])
    mine = butterfly_sum(mine, ("x", "yh"), sizes)
    other = lax.ppermute(mine, "c", [(0, 1), (1, 0)])
    low = jnp.where(first_core, mine, other)
    high = jnp.where(first_core, other, mine)
    own_sums = jnp.concatenate([low[:BLOCK], high[:BLOCK]], axis=0)
    own_total = low[BLOCK]
    own_scale = mass_ratio * lax.dynamic_slice_in_dim(cand_mass, own_start, local_cands) / own_total
    new_support = own_sums / own_total[:, None]
    return (ds_col.reshape(local_rows), own_scale, new_support)


def solution(mesh):
    row_size, col_size = mesh.devices.shape
    fine = Mesh(mesh.devices.reshape(2, row_size // 4, 2, col_size // 2, 2), ALL_AXES)
    sizes = dict(fine.shape)
    placed = (
        P(ALL_AXES, None),
        P(ALL_AXES),
        P(ALL_AXES, None),
        P(COL_AXES, None),
        P(),
    )
    return jax.shard_map(
        functools.partial(on_device, sizes),
        mesh=fine,
        in_specs=placed,
        out_specs=(P(ALL_AXES), P(COL_AXES), P(COL_AXES, None)),
        check_vma=False,
    )
```
